256 devices in a mesh: mode: 16 (over y, x), slab: 16 (over z, core).
Axes of the slice: x: 4, y: 4, z: 8, core: 2. Of those that a mesh axis runs over, the one named last changes fastest.
Arguments:
- velocity: float32 [3, 64, 256, 128], P(None, 'mode', 'slab'), may hold values from -6 to 6
- vorticity: bfloat16 [3, 64, 256, 128], P(None, 'mode', 'slab'), may hold values from -1.5 to 1.5
- lift: bfloat16 [4096, 1920], P('slab'), may hold values from -0.125 to 0.125
- extend: bfloat16 [30720, 256], P('slab'), may hold values from -0.375 to 0.375
- interface_chain_factors: float32 [2, 64, 2048, 128], P(None, 'mode', 'slab'), may hold values from -1 to 1
- pivot_inverse: float32 [64, 2048, 128], P('mode', 'slab'), may hold values from -1 to 1
- interior_diag: float32 [240, 128], P('slab'), may hold values from 0.5 to 4
- node_map: int32 [16, 256], P('slab'), may hold values from 0 to 127, as said below
Outputs:
- new_velocity: float32 [3, 64, 256, 128], P(None, 'mode', 'slab')
The draws below stay inside these ranges and needn't reach their ends.
Inputs may be any that keep to these rules, and one draw needn't show every extreme that they name: `node_map`: the first 128 and the last 128 entries of each row are each a permutation of 0 to 127.
All inputs are finite; a program needn't handle non-finite values.
Results may differ from the reference program's by a relative error of at most 0.0062.
Values may be sent and summed in bfloat16 or wider, within the bound.
No kernel may reach another device: no remote copies, remote signals or barrier semaphores. Data moves between devices by JAX's collectives and lax.ppermute only.
A program may use at most 128 MiB of HBM per device.

```python
import math
import jax
import jax.numpy as jnp
from jax import lax

PLANES = 64
POINTS = 128
LINES = 16
QUAD = 96
INTERIOR = 1920
LINES_ALL = 256
N_SLAB = 16


def loguniform_draw(key, array_extent, low, high):
    return jnp.exp(jax.random.uniform(key, array_extent, jnp.float32, math.log(low), math.log(high)))


def factor_stack(key, number_of_members):
    damping_speed_key, layer_key, stochastic_spike_key, magnitude_key, padding_key = jax.random.split(key, 5)
    damping_speeds = loguniform_draw(damping_speed_key, (number_of_members, PLANES, 1, POINTS, 1), 0.005, 2.0)
    layer_multiplier = loguniform_draw(layer_key, (number_of_members, 1, N_SLAB, 1, 1), 0.5, 2.0)
    lone_spike_height = jax.random.uniform(stochastic_spike_key, (number_of_members, 1, N_SLAB, 1, 1), jnp.float32)
    stochastic_spike_heights = jax.random.uniform(magnitude_key, (number_of_members, 1, N_SLAB, 1, 1), jnp.float32, 0.5, 0.8)
    stochastic_spike_amplitude = jnp.where(lone_spike_height < 0.15, stochastic_spike_heights, 1.0)
    pivot_submatrix = 0.95 * jnp.exp(-damping_speeds * layer_multiplier) * stochastic_spike_amplitude
    fill = jax.random.uniform(padding_key, (number_of_members, PLANES, N_SLAB, POINTS, POINTS), jnp.float32, -1.0, 1.0) * (0.5 / POINTS)
    return fill + jnp.eye(POINTS, dtype=jnp.float32) * pivot_submatrix


def draw_interface_chain_factors(key, part):
    stacked = factor_stack(jax.random.fold_in(key, 31), 2)
    return stacked.reshape(2, PLANES, N_SLAB * POINTS, POINTS)


def draw_pivot_inverse(key, part):
    gain_key, padding_key = jax.random.split(jax.random.fold_in(key, 37))
    gains = loguniform_draw(gain_key, (PLANES, N_SLAB, POINTS, 1), 0.15, 0.6)
    fill = jax.random.uniform(padding_key, (PLANES, N_SLAB, POINTS, POINTS), jnp.float32, -1.0, 1.0) * (0.16 / POINTS)
    blocks = fill + jnp.eye(POINTS, dtype=jnp.float32) * gains
    return blocks.reshape(PLANES, N_SLAB * POINTS, POINTS)


def node_block(layer_key):
    left_key, right_key = jax.random.split(layer_key)
    left_perm = jax.random.permutation(left_key, POINTS)
    right_perm = jax.random.permutation(right_key, POINTS)
    return jnp.concatenate([left_perm, right_perm]).astype(jnp.int32)


def draw_node_map(key, part):
    slab_keys = jax.random.split(jax.random.fold_in(key, 23), N_SLAB)
    return jax.vmap(node_block)(slab_keys)


def level_of(key, dims, cuts, least, top_value):
    level, own = 1.0, jax.random.fold_in(key, 6)
    for dim, parts in cuts:
        draws = jnp.exp(jax.random.uniform(jax.random.fold_in(own, dim), (parts,), jnp.float32, least / len(cuts), top_value / len(cuts)))
        level = level * jnp.repeat(draws, dims[dim] // parts).reshape([-1 if axis == dim else 1 for axis in range(len(dims))])
    return level


def normal_values(stream_key, dims, width, limit, shards=(), held_as=jnp.bfloat16):
    values = width * jax.random.normal(stream_key, dims, jnp.float32)
    if shards:
        values = values * level_of(stream_key, dims, shards, -0.22, 0.18)
    return jnp.clip(values, -limit, limit).astype(held_as)


def setup_inputs(seed: int = 0) -> dict:
    key_list = jax.random.split(jax.random.key(seed), 9)
    return {
        "velocity": normal_values(key_list[0], (3, PLANES, LINES_ALL, POINTS), 1.0, 6.0, ((1, 16), (2, 16)), jnp.float32),
        "vorticity": normal_values(key_list[1], (3, PLANES, LINES_ALL, POINTS), 0.1, 1.5, ((1, 16), (2, 16))),
        "lift": normal_values(key_list[2], (2 * POINTS * N_SLAB, INTERIOR), INTERIOR ** -0.5, 0.125, ((0, 16),)),
        "extend": normal_values(key_list[3], (INTERIOR * N_SLAB, 2 * POINTS), (2 * POINTS) ** -0.5, 0.375, ((0, 16),)),
        "interface_chain_factors": draw_interface_chain_factors(jax.random.fold_in(key_list[8], 71), 0),
        "pivot_inverse": draw_pivot_inverse(jax.random.fold_in(key_list[8], 71), 0),
        "interior_diag": jnp.clip(jnp.exp(math.log(4.0) - 2.0794415 * jax.random.uniform(key_list[6], ((LINES - 1) * N_SLAB, POINTS), jnp.float32) ** level_of(key_list[6], ((LINES - 1) * N_SLAB, POINTS), ((0, 16),), -0.2, 0.2)), 0.5, 4.0),
        "node_map": draw_node_map(jax.random.fold_in(key_list[8], 71), 0),
    }


LAMBDA_TIMESTEP = 0.5
WAVE_BASE = 0.125


def plane_numbers(planes):
    index_plane = jnp.arange(planes, dtype=jnp.int32)
    return jnp.where(index_plane == 1, planes // 2, index_plane // 2).astype(jnp.int32)


def plane_shift(wavenum):
    return LAMBDA_TIMESTEP + (wavenum.astype(jnp.float32) * WAVE_BASE) ** 2


def spectral_tables(planes, quad_points):
    wavenum = plane_numbers(planes)
    station = jnp.arange(quad_points, dtype=jnp.int32)
    phases = (station[:, None] * wavenum[None, :]) % quad_points
    angles = phases.astype(jnp.float32) * (2.0 * jnp.pi / quad_points)
    index_plane = jnp.arange(planes, dtype=jnp.int32)
    odd_plane = (index_plane % 2 == 1) & (index_plane != 1)
    inverse = jnp.where(odd_plane[None, :], -jnp.sin(angles), jnp.cos(angles))
    weights = jnp.where(index_plane == 0, 1.0, 2.0).astype(jnp.float32) / quad_points
    forward = weights[:, None] * inverse.T
    return inverse.astype(jnp.bfloat16), forward.astype(jnp.bfloat16)


def lamb_vector(velocity_phys, vorticity_phys):
    first = velocity_phys[1] * vorticity_phys[2] - velocity_phys[2] * vorticity_phys[1]
    second = velocity_phys[2] * vorticity_phys[0] - velocity_phys[0] * vorticity_phys[2]
    third = velocity_phys[0] * vorticity_phys[1] - velocity_phys[1] * vorticity_phys[0]
    return jnp.stack([first, second, third])


def block_application(blocks, vectors):
    return jnp.einsum("pab,pcb->pca", blocks, vectors, precision=lax.Precision.HIGHEST)


def reference(velocity, vorticity, lift, extend, interface_chain_factors, pivot_inverse, interior_diag, node_map):
    point_total = POINTS
    slab_count = N_SLAB
    highest = lax.Precision.HIGHEST
    inverse, forward = spectral_tables(PLANES, QUAD)
    shifts = plane_shift(plane_numbers(PLANES))
    velocity_half = velocity.astype(jnp.bfloat16)
    vel_phys = jnp.einsum("qp,cplb->cqlb", inverse.astype(jnp.float32), velocity_half.astype(jnp.float32), precision=highest)
    vort_phys = jnp.einsum("qp,cplb->cqlb", inverse.astype(jnp.float32), vorticity.astype(jnp.float32), precision=highest)
    lamb_field = lamb_vector(vel_phys, vort_phys).astype(jnp.bfloat16)
    nonlin = jnp.einsum("pq,cqlb->cplb", forward.astype(jnp.float32), lamb_field.astype(jnp.float32), precision=highest).astype(jnp.bfloat16)
    vel_slab = velocity.reshape(3, PLANES, slab_count, LINES, point_total)
    nonlin_slab = nonlin.reshape(3, PLANES, slab_count, LINES, point_total)
    rhs_zero = LAMBDA_TIMESTEP * vel_slab[:, :, :, 0, :] + nonlin_slab[:, :, :, 0, :].astype(jnp.float32)
    interior_point_velocity = (LAMBDA_TIMESTEP * vel_slab[:, :, :, 1:, :]).astype(jnp.bfloat16).reshape(3, PLANES, slab_count, INTERIOR)
    inner_nonlinear_term = nonlin_slab[:, :, :, 1:, :].reshape(3, PLANES, slab_count, INTERIOR)
    lift_slab = lift.reshape(slab_count, 2 * point_total, INTERIOR).astype(jnp.float32)
    condensed = jnp.einsum("sri,cpsi->pscr", lift_slab, interior_point_velocity.astype(jnp.float32), precision=highest)
    condensed = condensed + jnp.einsum("sri,cpsi->pscr", lift_slab, inner_nonlinear_term.astype(jnp.float32), precision=highest)
    halfway_offsets = jnp.concatenate([jnp.zeros((point_total,), jnp.int32), jnp.full((point_total,), point_total, jnp.int32)])
    row_order = (node_map + halfway_offsets[None, :]).astype(jnp.int32)
    cond_line = jnp.take_along_axis(condensed, row_order[None, :, None, :], axis=3)
    rhs_zero_planes = jnp.transpose(rhs_zero, (1, 2, 0, 3))
    rhs_left = cond_line[:, :, :, :point_total] + rhs_zero_planes
    rhs_right = cond_line[:, :, :, point_total:]
    interface_source = rhs_right[:, :-1] + rhs_left[:, 1:]
    factor_matrices = interface_chain_factors.reshape(2, PLANES, slab_count, point_total, point_total)
    elimination_matrices = jnp.swapaxes(factor_matrices[0, :, 1:], 0, 1)
    back_blocks = jnp.swapaxes(factor_matrices[1, :, 1:], 0, 1)
    pivot_blocks = jnp.swapaxes(pivot_inverse.reshape(PLANES, slab_count, point_total, point_total)[:, 1:], 0, 1)
    source_chain = jnp.swapaxes(interface_source, 0, 1)

    def forward_advance(preceding_entry, element_payload):
        elimination_single, source_block = element_payload
        current_entry = source_block - block_application(elimination_single, preceding_entry)
        return current_entry, current_entry

    initial_values = jnp.zeros((PLANES, 3, point_total), jnp.float32)
    discarded_final, forward_results = lax.scan(forward_advance, initial_values, (elimination_matrices, source_chain))

    def backward_step(after_value, element_payload):
        pivot_block, back_block, forward_value = element_payload
        current_entry = block_application(pivot_block, forward_value) - block_application(back_block, after_value)
        return current_entry, current_entry

    unused_first, interface_values = lax.scan(backward_step, initial_values, (pivot_blocks, back_blocks, forward_results), reverse=True)
    wall_rows = jnp.zeros((1, PLANES, 3, point_total), jnp.float32)
    interfaces = jnp.concatenate([wall_rows, interface_values, wall_rows], axis=0)
    boundary_line = jnp.concatenate([interfaces[:-1], interfaces[1:]], axis=3)
    boundary_line = jnp.transpose(boundary_line, (1, 0, 2, 3))
    inverse_order = jnp.argsort(row_order, axis=1).astype(jnp.int32)
    local_boundary_rows = jnp.take_along_axis(boundary_line, inverse_order[None, :, None, :], axis=3).astype(jnp.bfloat16)
    ext_slab = extend.reshape(slab_count, INTERIOR, 2 * point_total).astype(jnp.float32)
    extension = jnp.einsum("sir,pscr->cpsi", ext_slab, local_boundary_rows.astype(jnp.float32), precision=highest)
    extension = extension.reshape(3, PLANES, slab_count, LINES - 1, point_total)
    diag_slab = interior_diag.reshape(slab_count, LINES - 1, point_total)
    inner_rhs = LAMBDA_TIMESTEP * vel_slab[:, :, :, 1:, :] + nonlin_slab[:, :, :, 1:, :].astype(jnp.float32)
    new_inner = extension + inner_rhs / (diag_slab[None, None] + shifts[None, :, None, None, None])
    line_zero = jnp.transpose(interfaces[:-1], (2, 1, 0, 3))
    result = jnp.concatenate([line_zero[:, :, :, None, :], new_inner], axis=3)
    return result.reshape(3, PLANES, LINES_ALL, point_total)
```

```python
import jax
import jax.numpy as jnp
from jax import lax
from jax.sharding import PartitionSpec as P

PLANES = 64


LAMBDA_TIMESTEP = 0.5
WAVE_BASE = 0.125
HIGHEST = lax.Precision.HIGHEST


def plane_numbers(planes):
    index_plane = jnp.arange(planes, dtype=jnp.int32)
    return jnp.where(index_plane == 1, planes // 2, index_plane // 2)


def plane_shift(wavenum):
    return LAMBDA_TIMESTEP + (wavenum.astype(jnp.float32) * WAVE_BASE) ** 2


def spectral_tables(planes, quad_points):
    wavenum = plane_numbers(planes)
    station = jnp.arange(quad_points, dtype=jnp.int32)
    phases = station[:, None] * wavenum[None, :] % quad_points
    angles = phases.astype(jnp.float32) * (2.0 * jnp.pi / quad_points)
    index_plane = jnp.arange(planes, dtype=jnp.int32)
    odd_plane = (index_plane % 2 == 1) & (index_plane != 1)
    inverse = jnp.where(odd_plane[None, :], -jnp.sin(angles), jnp.cos(angles))
    weights = jnp.where(index_plane == 0, 1.0, 2.0).astype(jnp.float32) / quad_points
    forward = weights[:, None] * inverse.T
    return (inverse.astype(jnp.bfloat16), forward.astype(jnp.bfloat16))


def lamb_vector(velocity_phys, vorticity_phys):
    first = velocity_phys[1] * vorticity_phys[2] - velocity_phys[2] * vorticity_phys[1]
    second = velocity_phys[2] * vorticity_phys[0] - velocity_phys[0] * vorticity_phys[2]
    third = velocity_phys[0] * vorticity_phys[1] - velocity_phys[1] * vorticity_phys[0]
    return jnp.stack([first, second, third])


def mapping_application(matrix, vectors):
    return jnp.einsum("pab,pcb->pca", matrix, vectors, precision=HIGHEST)


def chain_stack(factors, start, first, last, step):
    count = factors.shape[0]
    slots = jnp.arange(count, dtype=jnp.int32)[:, None, None, None]
    eye = jnp.eye(factors.shape[-1], dtype=factors.dtype)
    stack = jnp.where((slots == start) & (start >= first) & (start <= last), eye, 0.0)
    stack = jnp.broadcast_to(stack, factors.shape)
    running = jnp.broadcast_to(eye, factors.shape[1:])

    def body(distance, carry):
        running, stack = carry
        target = start + step * distance
        factor = lax.dynamic_index_in_dim(
            factors, jnp.clip(target - step, 0, count - 1), 0, keepdims=False
        )
        running = jnp.einsum("pab,pbd->pad", running, factor, precision=HIGHEST)
        valid = (target >= first) & (target <= last)
        current = lax.dynamic_index_in_dim(stack, jnp.clip(target, 0, count - 1), 0, keepdims=False)
        stack = lax.dynamic_update_index_in_dim(
            stack, jnp.where(valid, running, current), jnp.clip(target, 0, count - 1), 0
        )
        return running, stack

    return lax.fori_loop(1, count, body, (running, stack))[1]


def on_device(
    velocity,
    vorticity,
    lift,
    extend,
    interface_chain_factors,
    pivot_inverse,
    interior_diag,
    node_map,
):
    components, planes_dev, line_count, point_total = velocity.shape
    quad_points = 3 * PLANES // 2
    slab_index = lax.axis_index("slab")
    slab_count = lax.axis_size("slab")

    factors = lax.all_gather(interface_chain_factors, "slab", axis=1)
    elimination_all = -factors[0]
    back_all = -factors[1]
    upstream = chain_stack(elimination_all, slab_index, 1, slab_count - 1, -1)
    downstream = chain_stack(back_all, slab_index + 1, 1, slab_count - 1, 1)

    halfway_offsets = jnp.concatenate(
        [jnp.zeros((point_total,), jnp.int32), jnp.full((point_total,), point_total, jnp.int32)]
    )
    row_order = node_map[0] + halfway_offsets
    one_hot = (
        row_order[:, None] == jnp.arange(2 * point_total, dtype=jnp.int32)[None, :]
    ).astype(jnp.bfloat16)
    lift_rows = jnp.einsum(
        "ir,rf->if", one_hot, lift, preferred_element_type=jnp.float32
    ).astype(jnp.bfloat16)
    extend_cols = jnp.einsum(
        "hr,ir->hi", extend, one_hot, preferred_element_type=jnp.float32
    ).astype(jnp.bfloat16)

    inverse, forward = spectral_tables(PLANES, quad_points)
    wavenum = lax.dynamic_slice_in_dim(
        plane_numbers(PLANES), lax.axis_index("mode") * planes_dev, planes_dev
    )
    shifts = plane_shift(wavenum)
    velocity_half = velocity.astype(jnp.bfloat16)
    both_fields = jnp.concatenate([velocity_half, vorticity], axis=0)
    field_lines = lax.all_to_all(both_fields, "mode", split_axis=2, concat_axis=1, tiled=True)
    phys = jnp.einsum("qp,cplb->cqlb", inverse, field_lines, preferred_element_type=jnp.float32)
    lamb_field = lamb_vector(phys[:components], phys[components:]).astype(jnp.bfloat16)
    nonlin_lines = jnp.einsum(
        "pq,cqlb->cplb", forward, lamb_field, preferred_element_type=jnp.float32
    ).astype(jnp.bfloat16)
    interior_point_velocity = (
        (LAMBDA_TIMESTEP * velocity[:, :, 1:, :])
        .astype(jnp.bfloat16)
        .reshape(components, planes_dev, -1)
    )
    lifted_velocity = jnp.einsum(
        "hf,vqf->qvh", lift_rows, interior_point_velocity, preferred_element_type=jnp.float32
    )
    nonlin = lax.all_to_all(nonlin_lines, "mode", split_axis=1, concat_axis=2, tiled=True)
    inner_nonlinear_term = nonlin[:, :, 1:, :].reshape(components, planes_dev, -1)
    cond_line = lifted_velocity + jnp.einsum(
        "hf,vqf->qvh", lift_rows, inner_nonlinear_term, preferred_element_type=jnp.float32
    )
    line_zero_rhs = jnp.swapaxes(
        LAMBDA_TIMESTEP * velocity[:, :, 0, :] + nonlin[:, :, 0, :].astype(jnp.float32), 0, 1
    )
    rhs_left = cond_line[:, :, :point_total] + line_zero_rhs
    right_part = cond_line[:, :, point_total:]

    sides = lax.all_gather(jnp.stack([rhs_left, right_part]), "slab")
    previous_right = jnp.concatenate([jnp.zeros_like(sides[:1, 1]), sides[:-1, 1]], axis=0)
    interface_rhs = sides[:, 0] + previous_right
    forward_results = jnp.einsum("kpab,kpcb->pca", upstream, interface_rhs, precision=HIGHEST)
    pivot_term = mapping_application(pivot_inverse, forward_results)

    pivots = lax.all_gather(pivot_term, "slab")
    right_values = jnp.einsum("kpab,kpcb->pca", downstream, pivots, precision=HIGHEST)
    left_solved = pivot_term - mapping_application(interface_chain_factors[1], right_values)
    leading_flag = slab_index == 0
    left_values = jnp.where(leading_flag, 0.0, left_solved)

    boundary_line = jnp.concatenate([left_values, right_values], axis=2).astype(jnp.bfloat16)
    extension = jnp.einsum(
        "hg,dog->odh", extend_cols, boundary_line, preferred_element_type=jnp.float32
    )
    extension = extension.reshape(components, planes_dev, line_count - 1, point_total)
    inner_rhs = LAMBDA_TIMESTEP * velocity[:, :, 1:, :] + nonlin[:, :, 1:, :].astype(jnp.float32)
    new_inner = extension + inner_rhs / (interior_diag[None, None] + shifts[None, :, None, None])
    line_zero = jnp.swapaxes(left_values, 0, 1)
    return jnp.concatenate([line_zero[:, :, None, :], new_inner], axis=2)


def solution(mesh):
    in_specs = (
        P(None, "mode", "slab", None),
        P(None, "mode", "slab", None),
        P("slab", None),
        P("slab", None),
        P(None, "mode", "slab", None),
        P("mode", "slab", None),
        P("slab", None),
        P("slab", None),
    )
    out_specs = P(None, "mode", "slab", None)
    return jax.shard_map(
        on_device, mesh=mesh, in_specs=in_specs, out_specs=out_specs, check_vma=False
    )
```

```python
import functools

import jax
import jax.numpy as jnp
from jax import lax
from jax.sharding import PartitionSpec as P

PLANES = 64


LAMBDA_TIMESTEP = 0.5
WAVE_BASE = 0.125
HIGHEST = lax.Precision.HIGHEST


def plane_numbers(planes):
    index_plane = jnp.arange(planes, dtype=jnp.int32)
    return jnp.where(index_plane == 1, planes // 2, index_plane // 2)


def plane_shift(wavenum):
    return LAMBDA_TIMESTEP + (wavenum.astype(jnp.float32) * WAVE_BASE) ** 2


def spectral_tables(planes, quad_points):
    wavenum = plane_numbers(planes)
    station = jnp.arange(quad_points, dtype=jnp.int32)
    phases = station[:, None] * wavenum[None, :] % quad_points
    angles = phases.astype(jnp.float32) * (2.0 * jnp.pi / quad_points)
    index_plane = jnp.arange(planes, dtype=jnp.int32)
    odd_plane = (index_plane % 2 == 1) & (index_plane != 1)
    inverse = jnp.where(odd_plane[None, :], -jnp.sin(angles), jnp.cos(angles))
    weights = jnp.where(index_plane == 0, 1.0, 2.0).astype(jnp.float32) / quad_points
    forward = weights[:, None] * inverse.T
    return (inverse.astype(jnp.bfloat16), forward.astype(jnp.bfloat16))


def lamb_vector(velocity_phys, vorticity_phys):
    first = velocity_phys[1] * vorticity_phys[2] - velocity_phys[2] * vorticity_phys[1]
    second = velocity_phys[2] * vorticity_phys[0] - velocity_phys[0] * vorticity_phys[2]
    third = velocity_phys[0] * vorticity_phys[1] - velocity_phys[1] * vorticity_phys[0]
    return jnp.stack([first, second, third])


def owner_solve(blocks, sides, slab_count):
    zero = jnp.zeros_like(sides[0, 0])
    forward_values = [zero]
    for k in range(1, slab_count):
        source = sides[k, 0] + sides[k - 1, 1]
        applied = jnp.einsum("ab,cb->ca", blocks[k, 0], forward_values[-1], precision=HIGHEST)
        forward_values.append(source - applied)
    solved = [zero] * (slab_count + 1)
    for k in range(slab_count - 1, 0, -1):
        pivot = jnp.einsum("ab,cb->ca", blocks[k, 2], forward_values[k], precision=HIGHEST)
        back = jnp.einsum("ab,cb->ca", blocks[k, 1], solved[k + 1], precision=HIGHEST)
        solved[k] = pivot - back
    return jnp.stack(solved)


def on_device(
    velocity,
    vorticity,
    lift,
    extend,
    interface_chain_factors,
    pivot_inverse,
    interior_diag,
    node_map,
    *,
    slab_count,
):
    components, planes_dev, line_count, point_total = velocity.shape
    quad_points = 3 * PLANES // 2
    slab_index = lax.axis_index("slab")
    group_size = planes_dev
    group_count = slab_count // group_size
    position = slab_index % group_size
    owners = [plane * group_size + plane for plane in range(planes_dev)]

    blocks = jnp.stack(
        [interface_chain_factors[0], interface_chain_factors[1], pivot_inverse], axis=1
    )
    within = [blocks[position]]
    for offset in range(1, group_size):
        pairs = [
            (group * group_size + spot, group * group_size + (spot - offset) % group_size)
            for group in range(group_count)
            for spot in range(group_size)
        ]
        within.append(lax.ppermute(blocks[(position - offset) % group_size], "slab", pairs))
    group_blocks = jnp.roll(jnp.stack(within), position, axis=0)
    across = [group_blocks]
    for offset in range(1, group_count):
        pairs = [
            (((plane + offset) % group_count) * group_size + plane, owners[plane])
            for plane in range(planes_dev)
        ]
        across.append(lax.ppermute(group_blocks, "slab", pairs))
    plane_blocks = jnp.roll(jnp.stack(across), position, axis=0).reshape(
        (slab_count,) + blocks.shape[1:]
    )

    halfway_offsets = jnp.concatenate(
        [jnp.zeros((point_total,), jnp.int32), jnp.full((point_total,), point_total, jnp.int32)]
    )
    row_order = node_map[0] + halfway_offsets
    one_hot = (
        row_order[:, None] == jnp.arange(2 * point_total, dtype=jnp.int32)[None, :]
    ).astype(jnp.bfloat16)
    lift_rows = jnp.einsum(
        "ir,rf->if", one_hot, lift, preferred_element_type=jnp.float32
    ).astype(jnp.bfloat16)
    extend_cols = jnp.einsum(
        "hr,ir->hi", extend, one_hot, preferred_element_type=jnp.float32
    ).astype(jnp.bfloat16)

    inverse, forward = spectral_tables(PLANES, quad_points)
    wavenum = lax.dynamic_slice_in_dim(
        plane_numbers(PLANES), lax.axis_index("mode") * planes_dev, planes_dev
    )
    shifts = plane_shift(wavenum)
    velocity_half = velocity.astype(jnp.bfloat16)
    both_fields = jnp.concatenate([velocity_half, vorticity], axis=0)
    field_lines = lax.all_to_all(both_fields, "mode", split_axis=2, concat_axis=1, tiled=True)
    phys = jnp.einsum("qp,cplb->cqlb", inverse, field_lines, preferred_element_type=jnp.float32)
    lamb_field = lamb_vector(phys[:components], phys[components:]).astype(jnp.bfloat16)
    nonlin_lines = jnp.einsum(
        "pq,cqlb->cplb", forward, lamb_field, preferred_element_type=jnp.float32
    ).astype(jnp.bfloat16)
    interior_point_velocity = (
        (LAMBDA_TIMESTEP * velocity[:, :, 1:, :])
        .astype(jnp.bfloat16)
        .reshape(components, planes_dev, -1)
    )
    lifted_velocity = jnp.einsum(
        "hf,vqf->qvh", lift_rows, interior_point_velocity, preferred_element_type=jnp.float32
    )
    nonlin = lax.all_to_all(nonlin_lines, "mode", split_axis=1, concat_axis=2, tiled=True)
    inner_nonlinear_term = nonlin[:, :, 1:, :].reshape(components, planes_dev, -1)
    cond_line = lifted_velocity + jnp.einsum(
        "hf,vqf->qvh", lift_rows, inner_nonlinear_term, preferred_element_type=jnp.float32
    )
    line_zero_rhs = jnp.swapaxes(
        LAMBDA_TIMESTEP * velocity[:, :, 0, :] + nonlin[:, :, 0, :].astype(jnp.float32), 0, 1
    )
    rhs_left = cond_line[:, :, :point_total] + line_zero_rhs
    right_part = cond_line[:, :, point_total:]

    sides = jnp.stack([rhs_left, right_part], axis=1)
    destination_plane = jnp.asarray(
        [owners.index(slab) if slab in owners else 0 for slab in range(slab_count)], jnp.int32
    )
    to_owner = lax.all_to_all(
        sides[destination_plane], "slab", split_axis=0, concat_axis=0, tiled=True
    )
    solved = owner_solve(plane_blocks, to_owner, slab_count)
    both_sides = jnp.stack([solved[:-1], solved[1:]], axis=1)
    from_owner = lax.all_to_all(both_sides, "slab", split_axis=0, concat_axis=0, tiled=True)
    mine = from_owner[jnp.asarray(owners)]
    left_values = mine[:, 0]
    right_values = mine[:, 1]

    boundary_line = jnp.concatenate([left_values, right_values], axis=2).astype(jnp.bfloat16)
    extension = jnp.einsum(
        "hg,dog->odh", extend_cols, boundary_line, preferred_element_type=jnp.float32
    )
    extension = extension.reshape(components, planes_dev, line_count - 1, point_total)
    inner_rhs = LAMBDA_TIMESTEP * velocity[:, :, 1:, :] + nonlin[:, :, 1:, :].astype(jnp.float32)
    new_inner = extension + inner_rhs / (interior_diag[None, None] + shifts[None, :, None, None])
    line_zero = jnp.swapaxes(left_values, 0, 1)
    return jnp.concatenate([line_zero[:, :, None, :], new_inner], axis=2)


def solution(mesh):
    in_specs = (
        P(None, "mode", "slab", None),
        P(None, "mode", "slab", None),
        P("slab", None),
        P("slab", None),
        P(None, "mode", "slab", None),
        P("mode", "slab", None),
        P("slab", None),
        P("slab", None),
    )
    out_specs = P(None, "mode", "slab", None)
    return jax.shard_map(
        functools.partial(on_device, slab_count=mesh.shape["slab"]), mesh=mesh, in_specs=in_specs, out_specs=out_specs, check_vma=False
    )
```

```python
import functools

import jax
import jax.numpy as jnp
from jax import lax
from jax.experimental import pallas as pl
from jax.experimental.pallas import tpu as pltpu
from jax.sharding import PartitionSpec as P

PLANES = 64


LAMBDA_TIMESTEP = 0.5
WAVE_BASE = 0.125
HIGHEST = lax.Precision.HIGHEST


def plane_numbers(planes):
    index_plane = jnp.arange(planes, dtype=jnp.int32)
    return jnp.where(index_plane == 1, planes // 2, index_plane // 2)


def plane_shift(wavenum):
    return LAMBDA_TIMESTEP + (wavenum.astype(jnp.float32) * WAVE_BASE) ** 2


def spectral_tables(planes, quad_points):
    wavenum = plane_numbers(planes)
    station = jnp.arange(quad_points, dtype=jnp.int32)
    phases = station[:, None] * wavenum[None, :] % quad_points
    angles = phases.astype(jnp.float32) * (2.0 * jnp.pi / quad_points)
    index_plane = jnp.arange(planes, dtype=jnp.int32)
    odd_plane = (index_plane % 2 == 1) & (index_plane != 1)
    inverse = jnp.where(odd_plane[None, :], -jnp.sin(angles), jnp.cos(angles))
    weights = jnp.where(index_plane == 0, 1.0, 2.0).astype(jnp.float32) / quad_points
    forward = weights[:, None] * inverse.T
    return (inverse.astype(jnp.bfloat16), forward.astype(jnp.bfloat16))


def lamb_vector(velocity_phys, vorticity_phys):
    first = velocity_phys[1] * vorticity_phys[2] - velocity_phys[2] * vorticity_phys[1]
    second = velocity_phys[2] * vorticity_phys[0] - velocity_phys[0] * vorticity_phys[2]
    third = velocity_phys[0] * vorticity_phys[1] - velocity_phys[1] * vorticity_phys[0]
    return jnp.stack([first, second, third])


def chain_kernel(position_ref, blocks_ref, sides_ref, out_ref, *, group_size):
    slab_count = sides_ref.shape[0]
    position = position_ref[0]

    def slot(slab):
        group_slot = (slab // group_size - position + group_size) % group_size
        spot_slot = (slab % group_size - position + group_size) % group_size
        return group_slot * group_size + spot_slot

    def apply(matrix, vectors):
        return lax.dot_general(
            vectors,
            matrix,
            (((1,), (1,)), ((), ())),
            precision=HIGHEST,
            preferred_element_type=jnp.float32,
        )

    zero = jnp.zeros(sides_ref.shape[2:], jnp.float32)
    forward_values = [zero]
    for k in range(1, slab_count):
        source = sides_ref[k, 0] + sides_ref[k - 1, 1]
        forward_values.append(source - apply(blocks_ref[slot(k), 0], forward_values[-1]))
    after = zero
    for k in range(slab_count - 1, 0, -1):
        blocks = blocks_ref[slot(k)]
        solved = apply(blocks[2], forward_values[k]) - apply(blocks[1], after)
        out_ref[k, 0] = solved
        out_ref[k, 1] = after
        after = solved
    out_ref[0, 0] = zero
    out_ref[0, 1] = after


def on_device(
    velocity,
    vorticity,
    lift,
    extend,
    interface_chain_factors,
    pivot_inverse,
    interior_diag,
    node_map,
    *,
    slab_count,
):
    components, planes_dev, line_count, point_total = velocity.shape
    quad_points = 3 * PLANES // 2
    slab_index = lax.axis_index("slab")
    group_size = planes_dev
    group_count = slab_count // group_size
    position = slab_index % group_size
    owners = [plane * group_size + plane for plane in range(planes_dev)]

    blocks = jnp.stack(
        [interface_chain_factors[0], interface_chain_factors[1], pivot_inverse], axis=1
    )
    within = [blocks[position]]
    for offset in range(1, group_size):
        pairs = [
            (group * group_size + spot, group * group_size + (spot - offset) % group_size)
            for group in range(group_count)
            for spot in range(group_size)
        ]
        within.append(lax.ppermute(blocks[(position - offset) % group_size], "slab", pairs))
    group_blocks = jnp.stack(within)
    across = [group_blocks]
    for offset in range(1, group_count):
        pairs = [
            (((plane + offset) % group_count) * group_size + plane, owners[plane])
            for plane in range(planes_dev)
        ]
        across.append(lax.ppermute(group_blocks, "slab", pairs))
    plane_blocks = jnp.concatenate(across, axis=0)

    halfway_offsets = jnp.concatenate(
        [jnp.zeros((point_total,), jnp.int32), jnp.full((point_total,), point_total, jnp.int32)]
    )
    row_order = node_map[0] + halfway_offsets
    one_hot = (
        row_order[:, None] == jnp.arange(2 * point_total, dtype=jnp.int32)[None, :]
    ).astype(jnp.bfloat16)
    lift_rows = jnp.einsum(
        "ir,rf->if", one_hot, lift, preferred_element_type=jnp.float32
    ).astype(jnp.bfloat16)
    extend_cols = jnp.einsum(
        "hr,ir->hi", extend, one_hot, preferred_element_type=jnp.float32
    ).astype(jnp.bfloat16)

    inverse, forward = spectral_tables(PLANES, quad_points)
    wavenum = lax.dynamic_slice_in_dim(
        plane_numbers(PLANES), lax.axis_index("mode") * planes_dev, planes_dev
    )
    shifts = plane_shift(wavenum)
    velocity_half = velocity.astype(jnp.bfloat16)
    both_fields = jnp.concatenate([velocity_half, vorticity], axis=0)
    field_lines = lax.all_to_all(both_fields, "mode", split_axis=2, concat_axis=1, tiled=True)
    phys = jnp.einsum("qp,cplb->cqlb", inverse, field_lines, preferred_element_type=jnp.float32)
    lamb_field = lamb_vector(phys[:components], phys[components:]).astype(jnp.bfloat16)
    nonlin_lines = jnp.einsum(
        "pq,cqlb->cplb", forward, lamb_field, preferred_element_type=jnp.float32
    ).astype(jnp.bfloat16)
    interior_point_velocity = (
        (LAMBDA_TIMESTEP * velocity[:, :, 1:, :])
        .astype(jnp.bfloat16)
        .reshape(components, planes_dev, -1)
    )
    lifted_velocity = jnp.einsum(
        "hf,vqf->qvh", lift_rows, interior_point_velocity, preferred_element_type=jnp.float32
    )
    nonlin = lax.all_to_all(nonlin_lines, "mode", split_axis=1, concat_axis=2, tiled=True)
    inner_nonlinear_term = nonlin[:, :, 1:, :].reshape(components, planes_dev, -1)
    cond_line = lifted_velocity + jnp.einsum(
        "hf,vqf->qvh", lift_rows, inner_nonlinear_term, preferred_element_type=jnp.float32
    )
    line_zero_rhs = jnp.swapaxes(
        LAMBDA_TIMESTEP * velocity[:, :, 0, :] + nonlin[:, :, 0, :].astype(jnp.float32), 0, 1
    )
    rhs_left = cond_line[:, :, :point_total] + line_zero_rhs
    right_part = cond_line[:, :, point_total:]

    sides = jnp.stack([rhs_left, right_part], axis=1)
    destination_plane = jnp.asarray(
        [owners.index(slab) if slab in owners else 0 for slab in range(slab_count)], jnp.int32
    )
    to_owner = lax.all_to_all(
        sides[destination_plane], "slab", split_axis=0, concat_axis=0, tiled=True
    )
    both_sides = pl.pallas_call(
        functools.partial(chain_kernel, group_size=group_size),
        out_shape=jax.ShapeDtypeStruct(to_owner.shape, jnp.float32),
        in_specs=[
            pl.BlockSpec(memory_space=pltpu.SMEM),
            pl.BlockSpec(memory_space=pltpu.VMEM),
            pl.BlockSpec(memory_space=pltpu.VMEM),
        ],
        out_specs=pl.BlockSpec(memory_space=pltpu.VMEM),
    )(position.astype(jnp.int32).reshape(1), plane_blocks, to_owner)
    from_owner = lax.all_to_all(both_sides, "slab", split_axis=0, concat_axis=0, tiled=True)
    mine = from_owner[jnp.asarray(owners)]
    left_values = mine[:, 0]
    right_values = mine[:, 1]

    boundary_line = jnp.concatenate([left_values, right_values], axis=2).astype(jnp.bfloat16)
    extension = jnp.einsum(
        "hg,dog->odh", extend_cols, boundary_line, preferred_element_type=jnp.float32
    )
    extension = extension.reshape(components, planes_dev, line_count - 1, point_total)
    inner_rhs = LAMBDA_TIMESTEP * velocity[:, :, 1:, :] + nonlin[:, :, 1:, :].astype(jnp.float32)
    new_inner = extension + inner_rhs / (interior_diag[None, None] + shifts[None, :, None, None])
    line_zero = jnp.swapaxes(left_values, 0, 1)
    return jnp.concatenate([line_zero[:, :, None, :], new_inner], axis=2)


def solution(mesh):
    in_specs = (
        P(None, "mode", "slab", None),
        P(None, "mode", "slab", None),
        P("slab", None),
        P("slab", None),
        P(None, "mode", "slab", None),
        P("mode", "slab", None),
        P("slab", None),
        P("slab", None),
    )
    out_specs = P(None, "mode", "slab", None)
    return jax.shard_map(
        functools.partial(on_device, slab_count=mesh.shape["slab"]), mesh=mesh, in_specs=in_specs, out_specs=out_specs, check_vma=False
    )
```

```python
import functools

import jax
import jax.numpy as jnp
from jax import lax
from jax.experimental import pallas as pl
from jax.experimental.pallas import tpu as pltpu
from jax.sharding import PartitionSpec as P

PLANES = 64


LAMBDA_TIMESTEP = 0.5
WAVE_BASE = 0.125
HIGHEST = lax.Precision.HIGHEST


def plane_numbers(planes):
    index_plane = jnp.arange(planes, dtype=jnp.int32)
    return jnp.where(index_plane == 1, planes // 2, index_plane // 2)


def plane_shift(wavenum):
    return LAMBDA_TIMESTEP + (wavenum.astype(jnp.float32) * WAVE_BASE) ** 2


def spectral_tables(planes, quad_points):
    wavenum = plane_numbers(planes)
    station = jnp.arange(quad_points, dtype=jnp.int32)
    phases = station[:, None] * wavenum[None, :] % quad_points
    angles = phases.astype(jnp.float32) * (2.0 * jnp.pi / quad_points)
    index_plane = jnp.arange(planes, dtype=jnp.int32)
    odd_plane = (index_plane % 2 == 1) & (index_plane != 1)
    inverse = jnp.where(odd_plane[None, :], -jnp.sin(angles), jnp.cos(angles))
    weights = jnp.where(index_plane == 0, 1.0, 2.0).astype(jnp.float32) / quad_points
    forward = weights[:, None] * inverse.T
    return (inverse.astype(jnp.bfloat16), forward.astype(jnp.bfloat16))


def lamb_vector(velocity_phys, vorticity_phys):
    first = velocity_phys[1] * vorticity_phys[2] - velocity_phys[2] * vorticity_phys[1]
    second = velocity_phys[2] * vorticity_phys[0] - velocity_phys[0] * vorticity_phys[2]
    third = velocity_phys[0] * vorticity_phys[1] - velocity_phys[1] * vorticity_phys[0]
    return jnp.stack([first, second, third])


def chain_kernel(position_ref, blocks_ref, sides_ref, out_ref, *, group_size):
    slab_count = sides_ref.shape[0]
    position = position_ref[0]

    def slot(slab):
        group_slot = (slab // group_size - position + group_size) % group_size
        spot_slot = (slab % group_size - position + group_size) % group_size
        return group_slot * group_size + spot_slot

    def apply(matrix, vectors):
        return lax.dot_general(
            vectors,
            matrix,
            (((1,), (1,)), ((), ())),
            precision=HIGHEST,
            preferred_element_type=jnp.float32,
        )

    zero = jnp.zeros(sides_ref.shape[2:], jnp.float32)
    forward_values = [zero]
    for k in range(1, slab_count):
        source = sides_ref[k, 0] + sides_ref[k - 1, 1]
        forward_values.append(source - apply(blocks_ref[slot(k), 0], forward_values[-1]))
    after = zero
    for k in range(slab_count - 1, 0, -1):
        blocks = blocks_ref[slot(k)]
        solved = apply(blocks[2], forward_values[k]) - apply(blocks[1], after)
        out_ref[k, 0] = solved
        out_ref[k, 1] = after
        after = solved
    out_ref[0, 0] = zero
    out_ref[0, 1] = after


def on_device(
    velocity,
    vorticity,
    lift,
    extend,
    interface_chain_factors,
    pivot_inverse,
    interior_diag,
    node_map,
    *,
    slab_count,
):
    components, planes_dev, line_count, point_total = velocity.shape
    quad_points = 3 * PLANES // 2
    slab_index = lax.axis_index("slab")
    group_size = planes_dev
    group_count = slab_count // group_size
    position = slab_index % group_size
    owners = [plane * group_size + plane for plane in range(planes_dev)]

    blocks = jnp.stack(
        [interface_chain_factors[0], interface_chain_factors[1], pivot_inverse], axis=1
    )
    within = [blocks[position]]
    for offset in range(1, group_size):
        pairs = [
            (group * group_size + spot, group * group_size + (spot - offset) % group_size)
            for group in range(group_count)
            for spot in range(group_size)
        ]
        within.append(lax.ppermute(blocks[(position - offset) % group_size], "slab", pairs))
    group_blocks = jnp.stack(within)

    halfway_offsets = jnp.concatenate(
        [jnp.zeros((point_total,), jnp.int32), jnp.full((point_total,), point_total, jnp.int32)]
    )
    row_order = node_map[0] + halfway_offsets
    one_hot = (
        row_order[:, None] == jnp.arange(2 * point_total, dtype=jnp.int32)[None, :]
    ).astype(jnp.bfloat16)
    lift_rows = jnp.einsum(
        "ir,rf->if", one_hot, lift, preferred_element_type=jnp.float32
    ).astype(jnp.bfloat16)
    extend_cols = jnp.einsum(
        "hr,ir->hi", extend, one_hot, preferred_element_type=jnp.float32
    ).astype(jnp.bfloat16)

    inverse, forward = spectral_tables(PLANES, quad_points)
    wavenum = lax.dynamic_slice_in_dim(
        plane_numbers(PLANES), lax.axis_index("mode") * planes_dev, planes_dev
    )
    shifts = plane_shift(wavenum)
    velocity_half = velocity.astype(jnp.bfloat16)
    both_fields = jnp.concatenate([velocity_half, vorticity], axis=0)
    field_lines = lax.all_to_all(both_fields, "mode", split_axis=2, concat_axis=1, tiled=True)
    group_blocks, field_lines = lax.optimization_barrier((group_blocks, field_lines))
    across = [group_blocks]
    for offset in range(1, group_count):
        pairs = [
            (((plane + offset) % group_count) * group_size + plane, owners[plane])
            for plane in range(planes_dev)
        ]
        across.append(lax.ppermute(group_blocks, "slab", pairs))
    plane_blocks = jnp.concatenate(across, axis=0)
    phys = jnp.einsum("qp,cplb->cqlb", inverse, field_lines, preferred_element_type=jnp.float32)
    lamb_field = lamb_vector(phys[:components], phys[components:]).astype(jnp.bfloat16)
    nonlin_lines = jnp.einsum(
        "pq,cqlb->cplb", forward, lamb_field, preferred_element_type=jnp.float32
    ).astype(jnp.bfloat16)
    interior_point_velocity = (
        (LAMBDA_TIMESTEP * velocity[:, :, 1:, :])
        .astype(jnp.bfloat16)
        .reshape(components, planes_dev, -1)
    )
    lifted_velocity = jnp.einsum(
        "hf,vqf->qvh", lift_rows, interior_point_velocity, preferred_element_type=jnp.float32
    )
    nonlin = lax.all_to_all(nonlin_lines, "mode", split_axis=1, concat_axis=2, tiled=True)
    inner_nonlinear_term = nonlin[:, :, 1:, :].reshape(components, planes_dev, -1)
    cond_line = lifted_velocity + jnp.einsum(
        "hf,vqf->qvh", lift_rows, inner_nonlinear_term, preferred_element_type=jnp.float32
    )
    line_zero_rhs = jnp.swapaxes(
        LAMBDA_TIMESTEP * velocity[:, :, 0, :] + nonlin[:, :, 0, :].astype(jnp.float32), 0, 1
    )
    rhs_left = cond_line[:, :, :point_total] + line_zero_rhs
    right_part = cond_line[:, :, point_total:]

    sides = jnp.stack([rhs_left, right_part], axis=1)
    destination_plane = jnp.asarray(
        [owners.index(slab) if slab in owners else 0 for slab in range(slab_count)], jnp.int32
    )
    to_owner = lax.all_to_all(
        sides[destination_plane], "slab", split_axis=0, concat_axis=0, tiled=True
    )
    both_sides = pl.pallas_call(
        functools.partial(chain_kernel, group_size=group_size),
        out_shape=jax.ShapeDtypeStruct(to_owner.shape, jnp.float32),
        in_specs=[
            pl.BlockSpec(memory_space=pltpu.SMEM),
            pl.BlockSpec(memory_space=pltpu.VMEM),
            pl.BlockSpec(memory_space=pltpu.VMEM),
        ],
        out_specs=pl.BlockSpec(memory_space=pltpu.VMEM),
    )(position.astype(jnp.int32).reshape(1), plane_blocks, to_owner)
    from_owner = lax.all_to_all(both_sides, "slab", split_axis=0, concat_axis=0, tiled=True)
    mine = from_owner[jnp.asarray(owners)]
    left_values = mine[:, 0]
    right_values = mine[:, 1]

    boundary_line = jnp.concatenate([left_values, right_values], axis=2).astype(jnp.bfloat16)
    extension = jnp.einsum(
        "hg,dog->odh", extend_cols, boundary_line, preferred_element_type=jnp.float32
    )
    extension = extension.reshape(components, planes_dev, line_count - 1, point_total)
    inner_rhs = LAMBDA_TIMESTEP * velocity[:, :, 1:, :] + nonlin[:, :, 1:, :].astype(jnp.float32)
    new_inner = extension + inner_rhs / (interior_diag[None, None] + shifts[None, :, None, None])
    line_zero = jnp.swapaxes(left_values, 0, 1)
    return jnp.concatenate([line_zero[:, :, None, :], new_inner], axis=2)


def solution(mesh):
    in_specs = (
        P(None, "mode", "slab", None),
        P(None, "mode", "slab", None),
        P("slab", None),
        P("slab", None),
        P(None, "mode", "slab", None),
        P("mode", "slab", None),
        P("slab", None),
        P("slab", None),
    )
    out_specs = P(None, "mode", "slab", None)
    return jax.shard_map(
        functools.partial(on_device, slab_count=mesh.shape["slab"]), mesh=mesh, in_specs=in_specs, out_specs=out_specs, check_vma=False
    )
```

```python
import functools

import jax
import jax.numpy as jnp
from jax import lax
from jax.experimental import pallas as pl
from jax.experimental.pallas import tpu as pltpu
from jax.sharding import PartitionSpec as P

PLANES = 64


LAMBDA_TIMESTEP = 0.5
WAVE_BASE = 0.125
HIGHEST = lax.Precision.HIGHEST


def plane_numbers(planes):
    index_plane = jnp.arange(planes, dtype=jnp.int32)
    return jnp.where(index_plane == 1, planes // 2, index_plane // 2)


def plane_shift(wavenum):
    return LAMBDA_TIMESTEP + (wavenum.astype(jnp.float32) * WAVE_BASE) ** 2


def spectral_tables(planes, quad_points):
    wavenum = plane_numbers(planes)
    station = jnp.arange(quad_points, dtype=jnp.int32)
    phases = station[:, None] * wavenum[None, :] % quad_points
    angles = phases.astype(jnp.float32) * (2.0 * jnp.pi / quad_points)
    index_plane = jnp.arange(planes, dtype=jnp.int32)
    odd_plane = (index_plane % 2 == 1) & (index_plane != 1)
    inverse = jnp.where(odd_plane[None, :], -jnp.sin(angles), jnp.cos(angles))
    weights = jnp.where(index_plane == 0, 1.0, 2.0).astype(jnp.float32) / quad_points
    forward = weights[:, None] * inverse.T
    return (inverse.astype(jnp.bfloat16), forward.astype(jnp.bfloat16))


def lamb_vector(velocity_phys, vorticity_phys):
    first = velocity_phys[1] * vorticity_phys[2] - velocity_phys[2] * vorticity_phys[1]
    second = velocity_phys[2] * vorticity_phys[0] - velocity_phys[0] * vorticity_phys[2]
    third = velocity_phys[0] * vorticity_phys[1] - velocity_phys[1] * vorticity_phys[0]
    return jnp.stack([first, second, third])


def chain_kernel(position_ref, *refs, group_size):
    group_refs = refs[:group_size]
    sides_ref, out_ref = refs[group_size:]
    slab_count = sides_ref.shape[0]

    def apply(matrix, vectors):
        return lax.dot_general(
            vectors,
            matrix,
            (((1,), (1,)), ((), ())),
            precision=HIGHEST,
            preferred_element_type=jnp.float32,
        )

    def solve(position):
        def blocks_of(slab):
            group_slot = (slab // group_size - position) % group_size
            spot_slot = (slab % group_size - position) % group_size
            return group_refs[group_slot].at[spot_slot]

        zero = jnp.zeros(sides_ref.shape[2:], jnp.float32)
        forward_values = [zero]
        for k in range(1, slab_count):
            source = sides_ref[k, 0] + sides_ref[k - 1, 1]
            forward_values.append(source - apply(blocks_of(k)[0], forward_values[-1]))
        after = zero
        for k in range(slab_count - 1, 0, -1):
            blocks = blocks_of(k)
            solved = apply(blocks[2], forward_values[k]) - apply(blocks[1], after)
            out_ref[k, 0] = solved
            out_ref[k, 1] = after
            after = solved
        out_ref[0, 0] = zero
        out_ref[0, 1] = after

    for position in range(group_size):
        pl.when(position_ref[0] == position)(functools.partial(solve, position))


def on_device(
    velocity,
    vorticity,
    lift,
    extend,
    interface_chain_factors,
    pivot_inverse,
    interior_diag,
    node_map,
    *,
    slab_count,
):
    components, planes_dev, line_count, point_total = velocity.shape
    quad_points = 3 * PLANES // 2
    slab_index = lax.axis_index("slab")
    group_size = planes_dev
    group_count = slab_count // group_size
    position = slab_index % group_size
    owners = [plane * group_size + plane for plane in range(planes_dev)]

    blocks = jnp.stack(
        [interface_chain_factors[0], interface_chain_factors[1], pivot_inverse], axis=1
    )
    within = [blocks[position]]
    for offset in range(1, group_size):
        pairs = [
            (group * group_size + spot, group * group_size + (spot - offset) % group_size)
            for group in range(group_count)
            for spot in range(group_size)
        ]
        within.append(lax.ppermute(blocks[(position - offset) % group_size], "slab", pairs))
    group_blocks = jnp.stack(within)

    halfway_offsets = jnp.concatenate(
        [jnp.zeros((point_total,), jnp.int32), jnp.full((point_total,), point_total, jnp.int32)]
    )
    row_order = node_map[0] + halfway_offsets
    one_hot = (
        row_order[:, None] == jnp.arange(2 * point_total, dtype=jnp.int32)[None, :]
    ).astype(jnp.bfloat16)
    lift_rows = jnp.einsum(
        "ir,rf->if", one_hot, lift, preferred_element_type=jnp.float32
    ).astype(jnp.bfloat16)
    extend_cols = jnp.einsum(
        "hr,ir->hi", extend, one_hot, preferred_element_type=jnp.float32
    ).astype(jnp.bfloat16)

    inverse, forward = spectral_tables(PLANES, quad_points)
    wavenum = lax.dynamic_slice_in_dim(
        plane_numbers(PLANES), lax.axis_index("mode") * planes_dev, planes_dev
    )
    shifts = plane_shift(wavenum)
    velocity_half = velocity.astype(jnp.bfloat16)
    both_fields = jnp.concatenate([velocity_half, vorticity], axis=0)
    field_lines = lax.all_to_all(both_fields, "mode", split_axis=2, concat_axis=1, tiled=True)
    group_blocks, field_lines = lax.optimization_barrier((group_blocks, field_lines))
    across = [group_blocks]
    for offset in range(1, group_count):
        pairs = [
            (((plane + offset) % group_count) * group_size + plane, owners[plane])
            for plane in range(planes_dev)
        ]
        across.append(lax.ppermute(group_blocks, "slab", pairs))
    phys = jnp.einsum("qp,cplb->cqlb", inverse, field_lines, preferred_element_type=jnp.float32)
    lamb_field = lamb_vector(phys[:components], phys[components:]).astype(jnp.bfloat16)
    nonlin_lines = jnp.einsum(
        "pq,cqlb->cplb", forward, lamb_field, preferred_element_type=jnp.float32
    ).astype(jnp.bfloat16)
    interior_point_velocity = (
        (LAMBDA_TIMESTEP * velocity[:, :, 1:, :])
        .astype(jnp.bfloat16)
        .reshape(components, planes_dev, -1)
    )
    lifted_velocity = jnp.einsum(
        "hf,vqf->qvh", lift_rows, interior_point_velocity, preferred_element_type=jnp.float32
    )
    nonlin = lax.all_to_all(nonlin_lines, "mode", split_axis=1, concat_axis=2, tiled=True)
    inner_nonlinear_term = nonlin[:, :, 1:, :].reshape(components, planes_dev, -1)
    cond_line = lifted_velocity + jnp.einsum(
        "hf,vqf->qvh", lift_rows, inner_nonlinear_term, preferred_element_type=jnp.float32
    )
    line_zero_rhs = jnp.swapaxes(
        LAMBDA_TIMESTEP * velocity[:, :, 0, :] + nonlin[:, :, 0, :].astype(jnp.float32), 0, 1
    )
    rhs_left = cond_line[:, :, :point_total] + line_zero_rhs
    right_part = cond_line[:, :, point_total:]

    sides = jnp.stack([rhs_left, right_part], axis=1)
    destination_plane = jnp.asarray(
        [owners.index(slab) if slab in owners else 0 for slab in range(slab_count)], jnp.int32
    )
    to_owner = lax.all_to_all(
        sides[destination_plane], "slab", split_axis=0, concat_axis=0, tiled=True
    )
    both_sides = pl.pallas_call(
        functools.partial(chain_kernel, group_size=group_size),
        out_shape=jax.ShapeDtypeStruct(to_owner.shape, jnp.float32),
        in_specs=[pl.BlockSpec(memory_space=pltpu.SMEM)]
        + [pl.BlockSpec(memory_space=pltpu.VMEM)] * (group_size + 1),
        out_specs=pl.BlockSpec(memory_space=pltpu.VMEM),
    )(position.astype(jnp.int32).reshape(1), *across, to_owner)
    from_owner = lax.all_to_all(both_sides, "slab", split_axis=0, concat_axis=0, tiled=True)
    mine = from_owner[jnp.asarray(owners)]
    left_values = mine[:, 0]
    right_values = mine[:, 1]

    boundary_line = jnp.concatenate([left_values, right_values], axis=2).astype(jnp.bfloat16)
    extension = jnp.einsum(
        "hg,dog->odh", extend_cols, boundary_line, preferred_element_type=jnp.float32
    )
    extension = extension.reshape(components, planes_dev, line_count - 1, point_total)
    inner_rhs = LAMBDA_TIMESTEP * velocity[:, :, 1:, :] + nonlin[:, :, 1:, :].astype(jnp.float32)
    new_inner = extension + inner_rhs / (interior_diag[None, None] + shifts[None, :, None, None])
    line_zero = jnp.swapaxes(left_values, 0, 1)
    return jnp.concatenate([line_zero[:, :, None, :], new_inner], axis=2)


def solution(mesh):
    in_specs = (
        P(None, "mode", "slab", None),
        P(None, "mode", "slab", None),
        P("slab", None),
        P("slab", None),
        P(None, "mode", "slab", None),
        P("mode", "slab", None),
        P("slab", None),
        P("slab", None),
    )
    out_specs = P(None, "mode", "slab", None)
    return jax.shard_map(
        functools.partial(on_device, slab_count=mesh.shape["slab"]), mesh=mesh, in_specs=in_specs, out_specs=out_specs, check_vma=False
    )
```

```python
import functools

import jax
import jax.numpy as jnp
from jax import lax
from jax.experimental import pallas as pl
from jax.experimental.pallas import tpu as pltpu
from jax.sharding import PartitionSpec as P

PLANES = 64


LAMBDA_TIMESTEP = 0.5
WAVE_BASE = 0.125
HIGHEST = lax.Precision.HIGHEST


def plane_numbers(planes):
    index_plane = jnp.arange(planes, dtype=jnp.int32)
    return jnp.where(index_plane == 1, planes // 2, index_plane // 2)


def plane_shift(wavenum):
    return LAMBDA_TIMESTEP + (wavenum.astype(jnp.float32) * WAVE_BASE) ** 2


def spectral_tables(planes, quad_points):
    wavenum = plane_numbers(planes)
    station = jnp.arange(quad_points, dtype=jnp.int32)
    phases = station[:, None] * wavenum[None, :] % quad_points
    angles = phases.astype(jnp.float32) * (2.0 * jnp.pi / quad_points)
    index_plane = jnp.arange(planes, dtype=jnp.int32)
    odd_plane = (index_plane % 2 == 1) & (index_plane != 1)
    inverse = jnp.where(odd_plane[None, :], -jnp.sin(angles), jnp.cos(angles))
    weights = jnp.where(index_plane == 0, 1.0, 2.0).astype(jnp.float32) / quad_points
    forward = weights[:, None] * inverse.T
    return (inverse.astype(jnp.bfloat16), forward.astype(jnp.bfloat16))


def lamb_vector(velocity_phys, vorticity_phys):
    first = velocity_phys[1] * vorticity_phys[2] - velocity_phys[2] * vorticity_phys[1]
    second = velocity_phys[2] * vorticity_phys[0] - velocity_phys[0] * vorticity_phys[2]
    third = velocity_phys[0] * vorticity_phys[1] - velocity_phys[1] * vorticity_phys[0]
    return jnp.stack([first, second, third])


def chain_kernel(position_ref, *refs, group_size):
    group_refs = refs[:group_size]
    sides_ref, out_ref = refs[group_size:]
    slab_count = sides_ref.shape[0]

    def apply(matrix, vectors):
        return lax.dot_general(
            vectors,
            matrix,
            (((1,), (1,)), ((), ())),
            precision=HIGHEST,
            preferred_element_type=jnp.float32,
        )

    def solve(position):
        def blocks_of(slab):
            group_slot = (slab // group_size - position) % group_size
            spot_slot = (slab % group_size - position) % group_size
            return group_refs[group_slot].at[spot_slot]

        zero = jnp.zeros(sides_ref.shape[2:], jnp.float32)
        forward_values = [zero]
        for k in range(1, slab_count):
            source = sides_ref[k, 0] + sides_ref[k - 1, 1]
            forward_values.append(source - apply(blocks_of(k)[0], forward_values[-1]))
        after = zero
        for k in range(slab_count - 1, 0, -1):
            blocks = blocks_of(k)
            solved = apply(blocks[2], forward_values[k]) - apply(blocks[1], after)
            out_ref[k, 0] = solved
            out_ref[k, 1] = after
            after = solved
        out_ref[0, 0] = zero
        out_ref[0, 1] = after

    for position in range(group_size):
        pl.when(position_ref[0] == position)(functools.partial(solve, position))


def on_device(
    velocity,
    vorticity,
    lift,
    extend,
    interface_chain_factors,
    pivot_inverse,
    interior_diag,
    node_map,
    *,
    slab_count,
):
    components, planes_dev, line_count, point_total = velocity.shape
    quad_points = 3 * PLANES // 2
    slab_index = lax.axis_index("slab")
    group_size = planes_dev
    group_count = slab_count // group_size
    position = slab_index % group_size
    owners = [plane * group_size + plane for plane in range(planes_dev)]

    blocks = jnp.stack(
        [interface_chain_factors[0], interface_chain_factors[1], pivot_inverse], axis=1
    )
    within = [blocks[position]]
    for offset in range(1, group_size):
        pairs = [
            (group * group_size + spot, group * group_size + (spot - offset) % group_size)
            for group in range(group_count)
            for spot in range(group_size)
        ]
        within.append(lax.ppermute(blocks[(position - offset) % group_size], "slab", pairs))
    group_blocks = jnp.stack(within)

    halfway_offsets = jnp.concatenate(
        [jnp.zeros((point_total,), jnp.int32), jnp.full((point_total,), point_total, jnp.int32)]
    )
    row_order = node_map[0] + halfway_offsets
    one_hot = (
        row_order[:, None] == jnp.arange(2 * point_total, dtype=jnp.int32)[None, :]
    ).astype(jnp.bfloat16)
    lift_rows = jnp.einsum(
        "ir,rf->if", one_hot, lift, preferred_element_type=jnp.float32
    ).astype(jnp.bfloat16)
    extend_cols = jnp.einsum(
        "hr,ir->hi", extend, one_hot, preferred_element_type=jnp.float32
    ).astype(jnp.bfloat16)

    inverse, forward = spectral_tables(PLANES, quad_points)
    wavenum = lax.dynamic_slice_in_dim(
        plane_numbers(PLANES), lax.axis_index("mode") * planes_dev, planes_dev
    )
    shifts = plane_shift(wavenum)
    velocity_half = velocity.astype(jnp.bfloat16)
    both_fields = jnp.concatenate([velocity_half, vorticity], axis=0)
    group_blocks, both_fields = lax.optimization_barrier((group_blocks, both_fields))
    field_lines = lax.all_to_all(both_fields, "mode", split_axis=2, concat_axis=1, tiled=True)
    across = [group_blocks]
    for offset in range(1, group_count):
        pairs = [
            (((plane + offset) % group_count) * group_size + plane, owners[plane])
            for plane in range(planes_dev)
        ]
        across.append(lax.ppermute(group_blocks, "slab", pairs))
    phys = jnp.einsum("qp,cplb->cqlb", inverse, field_lines, preferred_element_type=jnp.float32)
    lamb_field = lamb_vector(phys[:components], phys[components:]).astype(jnp.bfloat16)
    nonlin_lines = jnp.einsum(
        "pq,cqlb->cplb", forward, lamb_field, preferred_element_type=jnp.float32
    ).astype(jnp.bfloat16)
    interior_point_velocity = (
        (LAMBDA_TIMESTEP * velocity[:, :, 1:, :])
        .astype(jnp.bfloat16)
        .reshape(components, planes_dev, -1)
    )
    lifted_velocity = jnp.einsum(
        "hf,vqf->qvh", lift_rows, interior_point_velocity, preferred_element_type=jnp.float32
    )
    nonlin = lax.all_to_all(nonlin_lines, "mode", split_axis=1, concat_axis=2, tiled=True)
    inner_nonlinear_term = nonlin[:, :, 1:, :].reshape(components, planes_dev, -1)
    cond_line = lifted_velocity + jnp.einsum(
        "hf,vqf->qvh", lift_rows, inner_nonlinear_term, preferred_element_type=jnp.float32
    )
    line_zero_rhs = jnp.swapaxes(
        LAMBDA_TIMESTEP * velocity[:, :, 0, :] + nonlin[:, :, 0, :].astype(jnp.float32), 0, 1
    )
    rhs_left = cond_line[:, :, :point_total] + line_zero_rhs
    right_part = cond_line[:, :, point_total:]

    sides = jnp.stack([rhs_left, right_part], axis=1)
    destination_plane = jnp.asarray(
        [owners.index(slab) if slab in owners else 0 for slab in range(slab_count)], jnp.int32
    )
    to_owner = lax.all_to_all(
        sides[destination_plane], "slab", split_axis=0, concat_axis=0, tiled=True
    )
    both_sides = pl.pallas_call(
        functools.partial(chain_kernel, group_size=group_size),
        out_shape=jax.ShapeDtypeStruct(to_owner.shape, jnp.float32),
        in_specs=[pl.BlockSpec(memory_space=pltpu.SMEM)]
        + [pl.BlockSpec(memory_space=pltpu.VMEM)] * (group_size + 1),
        out_specs=pl.BlockSpec(memory_space=pltpu.VMEM),
    )(position.astype(jnp.int32).reshape(1), *across, to_owner)
    from_owner = lax.all_to_all(both_sides, "slab", split_axis=0, concat_axis=0, tiled=True)
    mine = from_owner[jnp.asarray(owners)]
    left_values = mine[:, 0]
    right_values = mine[:, 1]

    boundary_line = jnp.concatenate([left_values, right_values], axis=2).astype(jnp.bfloat16)
    extension = jnp.einsum(
        "hg,dog->odh", extend_cols, boundary_line, preferred_element_type=jnp.float32
    )
    extension = extension.reshape(components, planes_dev, line_count - 1, point_total)
    inner_rhs = LAMBDA_TIMESTEP * velocity[:, :, 1:, :] + nonlin[:, :, 1:, :].astype(jnp.float32)
    new_inner = extension + inner_rhs / (interior_diag[None, None] + shifts[None, :, None, None])
    line_zero = jnp.swapaxes(left_values, 0, 1)
    return jnp.concatenate([line_zero[:, :, None, :], new_inner], axis=2)


def solution(mesh):
    in_specs = (
        P(None, "mode", "slab", None),
        P(None, "mode", "slab", None),
        P("slab", None),
        P("slab", None),
        P(None, "mode", "slab", None),
        P("mode", "slab", None),
        P("slab", None),
        P("slab", None),
    )
    out_specs = P(None, "mode", "slab", None)
    return jax.shard_map(
        functools.partial(on_device, slab_count=mesh.shape["slab"]), mesh=mesh, in_specs=in_specs, out_specs=out_specs, check_vma=False
    )
```

```python
import functools

import jax
import jax.numpy as jnp
from jax import lax
from jax.experimental import pallas as pl
from jax.experimental.pallas import tpu as pltpu
from jax.sharding import PartitionSpec as P

PLANES = 64


LAMBDA_TIMESTEP = 0.5
WAVE_BASE = 0.125
HIGHEST = lax.Precision.HIGHEST


def plane_numbers(planes):
    index_plane = jnp.arange(planes, dtype=jnp.int32)
    return jnp.where(index_plane == 1, planes // 2, index_plane // 2)


def plane_shift(wavenum):
    return LAMBDA_TIMESTEP + (wavenum.astype(jnp.float32) * WAVE_BASE) ** 2


def spectral_tables(planes, quad_points):
    wavenum = plane_numbers(planes)
    station = jnp.arange(quad_points, dtype=jnp.int32)
    phases = station[:, None] * wavenum[None, :] % quad_points
    angles = phases.astype(jnp.float32) * (2.0 * jnp.pi / quad_points)
    index_plane = jnp.arange(planes, dtype=jnp.int32)
    odd_plane = (index_plane % 2 == 1) & (index_plane != 1)
    inverse = jnp.where(odd_plane[None, :], -jnp.sin(angles), jnp.cos(angles))
    weights = jnp.where(index_plane == 0, 1.0, 2.0).astype(jnp.float32) / quad_points
    forward = weights[:, None] * inverse.T
    return (inverse.astype(jnp.bfloat16), forward.astype(jnp.bfloat16))


def lamb_vector(velocity_phys, vorticity_phys):
    first = velocity_phys[1] * vorticity_phys[2] - velocity_phys[2] * vorticity_phys[1]
    second = velocity_phys[2] * vorticity_phys[0] - velocity_phys[0] * vorticity_phys[2]
    third = velocity_phys[0] * vorticity_phys[1] - velocity_phys[1] * vorticity_phys[0]
    return jnp.stack([first, second, third])


def chain_kernel(position_ref, *refs, group_size):
    group_refs = refs[:group_size]
    sides_ref, out_ref = refs[group_size:]
    slab_count = sides_ref.shape[0]

    def apply(matrix, vectors):
        return lax.dot_general(
            vectors,
            matrix,
            (((1,), (1,)), ((), ())),
            precision=HIGHEST,
            preferred_element_type=jnp.float32,
        )

    def solve(position):
        def blocks_of(slab):
            group_slot = (slab // group_size - position) % group_size
            spot_slot = (slab % group_size - position) % group_size
            return group_refs[group_slot].at[spot_slot]

        zero = jnp.zeros(sides_ref.shape[2:], jnp.float32)
        forward_values = [zero]
        for k in range(1, slab_count):
            source = sides_ref[k, 0] + sides_ref[k - 1, 1]
            forward_values.append(source - apply(blocks_of(k)[0], forward_values[-1]))
        after = zero
        for k in range(slab_count - 1, 0, -1):
            blocks = blocks_of(k)
            solved = apply(blocks[2], forward_values[k]) - apply(blocks[1], after)
            out_ref[k, 0] = solved
            out_ref[k, 1] = after
            after = solved
        out_ref[0, 0] = zero
        out_ref[0, 1] = after

    for position in range(group_size):
        pl.when(position_ref[0] == position)(functools.partial(solve, position))


def on_device(
    velocity,
    vorticity,
    lift,
    extend,
    interface_chain_factors,
    pivot_inverse,
    interior_diag,
    node_map,
    *,
    slab_count,
):
    components, planes_dev, line_count, point_total = velocity.shape
    quad_points = 3 * PLANES // 2
    slab_index = lax.axis_index("slab")
    group_size = planes_dev
    group_count = slab_count // group_size
    position = slab_index % group_size
    owners = [plane * group_size + plane for plane in range(planes_dev)]

    blocks = jnp.stack(
        [interface_chain_factors[0], interface_chain_factors[1], pivot_inverse], axis=1
    )
    within = [blocks[position]]
    for offset in range(1, group_size):
        pairs = [
            (group * group_size + spot, group * group_size + (spot - offset) % group_size)
            for group in range(group_count)
            for spot in range(group_size)
        ]
        within.append(lax.ppermute(blocks[(position - offset) % group_size], "slab", pairs))
    group_blocks = jnp.stack(within)

    halfway_offsets = jnp.concatenate(
        [jnp.zeros((point_total,), jnp.int32), jnp.full((point_total,), point_total, jnp.int32)]
    )
    row_order = node_map[0] + halfway_offsets
    one_hot = (
        row_order[:, None] == jnp.arange(2 * point_total, dtype=jnp.int32)[None, :]
    ).astype(jnp.bfloat16)
    lift_rows = jnp.einsum(
        "ir,rf->if", one_hot, lift, preferred_element_type=jnp.float32
    ).astype(jnp.bfloat16)
    extend_cols = jnp.einsum(
        "hr,ir->hi", extend, one_hot, preferred_element_type=jnp.float32
    ).astype(jnp.bfloat16)

    inverse, forward = spectral_tables(PLANES, quad_points)
    wavenum = lax.dynamic_slice_in_dim(
        plane_numbers(PLANES), lax.axis_index("mode") * planes_dev, planes_dev
    )
    shifts = plane_shift(wavenum)
    velocity_half = velocity.astype(jnp.bfloat16)
    both_fields = jnp.concatenate([velocity_half, vorticity], axis=0)
    field_lines = lax.all_to_all(both_fields, "mode", split_axis=2, concat_axis=1, tiled=True)
    group_blocks, field_lines = lax.optimization_barrier((group_blocks, field_lines))
    across = [group_blocks]
    for offset in range(1, group_count):
        pairs = [
            (((plane + offset) % group_count) * group_size + plane, owners[plane])
            for plane in range(planes_dev)
        ]
        across.append(lax.ppermute(group_blocks, "slab", pairs))
    phys = jnp.einsum("qp,cplb->cqlb", inverse, field_lines, preferred_element_type=jnp.float32)
    lamb_field = lamb_vector(phys[:components], phys[components:]).astype(jnp.bfloat16)
    nonlin_lines = jnp.einsum(
        "pq,cqlb->cplb", forward, lamb_field, preferred_element_type=jnp.float32
    ).astype(jnp.bfloat16)
    interior_point_velocity = (
        (LAMBDA_TIMESTEP * velocity[:, :, 1:, :])
        .astype(jnp.bfloat16)
        .reshape(components, planes_dev, -1)
    )
    lifted_velocity = jnp.einsum(
        "hf,vqf->qvh", lift_rows, interior_point_velocity, preferred_element_type=jnp.float32
    )
    nonlin = lax.all_to_all(nonlin_lines, "mode", split_axis=1, concat_axis=2, tiled=True)
    inner_nonlinear_term = nonlin[:, :, 1:, :].reshape(components, planes_dev, -1)
    cond_line = lifted_velocity + jnp.einsum(
        "hf,vqf->qvh", lift_rows, inner_nonlinear_term, preferred_element_type=jnp.float32
    )
    line_zero_rhs = jnp.swapaxes(
        LAMBDA_TIMESTEP * velocity[:, :, 0, :] + nonlin[:, :, 0, :].astype(jnp.float32), 0, 1
    )
    rhs_left = cond_line[:, :, :point_total] + line_zero_rhs
    right_part = cond_line[:, :, point_total:]

    sides = jnp.stack([rhs_left, right_part], axis=1)
    across, sides = lax.optimization_barrier((across, sides))
    destination_plane = jnp.asarray(
        [owners.index(slab) if slab in owners else 0 for slab in range(slab_count)], jnp.int32
    )
    to_owner = lax.all_to_all(
        sides[destination_plane], "slab", split_axis=0, concat_axis=0, tiled=True
    )
    both_sides = pl.pallas_call(
        functools.partial(chain_kernel, group_size=group_size),
        out_shape=jax.ShapeDtypeStruct(to_owner.shape, jnp.float32),
        in_specs=[pl.BlockSpec(memory_space=pltpu.SMEM)]
        + [pl.BlockSpec(memory_space=pltpu.VMEM)] * (group_size + 1),
        out_specs=pl.BlockSpec(memory_space=pltpu.VMEM),
    )(position.astype(jnp.int32).reshape(1), *across, to_owner)
    from_owner = lax.all_to_all(both_sides, "slab", split_axis=0, concat_axis=0, tiled=True)
    mine = from_owner[jnp.asarray(owners)]
    left_values = mine[:, 0]
    right_values = mine[:, 1]

    boundary_line = jnp.concatenate([left_values, right_values], axis=2).astype(jnp.bfloat16)
    extension = jnp.einsum(
        "hg,dog->odh", extend_cols, boundary_line, preferred_element_type=jnp.float32
    )
    extension = extension.reshape(components, planes_dev, line_count - 1, point_total)
    inner_rhs = LAMBDA_TIMESTEP * velocity[:, :, 1:, :] + nonlin[:, :, 1:, :].astype(jnp.float32)
    new_inner = extension + inner_rhs / (interior_diag[None, None] + shifts[None, :, None, None])
    line_zero = jnp.swapaxes(left_values, 0, 1)
    return jnp.concatenate([line_zero[:, :, None, :], new_inner], axis=2)


def solution(mesh):
    in_specs = (
        P(None, "mode", "slab", None),
        P(None, "mode", "slab", None),
        P("slab", None),
        P("slab", None),
        P(None, "mode", "slab", None),
        P("mode", "slab", None),
        P("slab", None),
        P("slab", None),
    )
    out_specs = P(None, "mode", "slab", None)
    return jax.shard_map(
        functools.partial(on_device, slab_count=mesh.shape["slab"]), mesh=mesh, in_specs=in_specs, out_specs=out_specs, check_vma=False
    )
```

```python
import functools

import jax
import jax.numpy as jnp
from jax import lax
from jax.experimental import pallas as pl
from jax.experimental.pallas import tpu as pltpu
from jax.sharding import PartitionSpec as P

PLANES = 64


LAMBDA_TIMESTEP = 0.5
WAVE_BASE = 0.125
HIGHEST = lax.Precision.HIGHEST


def plane_numbers(planes):
    index_plane = jnp.arange(planes, dtype=jnp.int32)
    return jnp.where(index_plane == 1, planes // 2, index_plane // 2)


def plane_shift(wavenum):
    return LAMBDA_TIMESTEP + (wavenum.astype(jnp.float32) * WAVE_BASE) ** 2


def spectral_tables(planes, quad_points):
    wavenum = plane_numbers(planes)
    station = jnp.arange(quad_points, dtype=jnp.int32)
    phases = station[:, None] * wavenum[None, :] % quad_points
    angles = phases.astype(jnp.float32) * (2.0 * jnp.pi / quad_points)
    index_plane = jnp.arange(planes, dtype=jnp.int32)
    odd_plane = (index_plane % 2 == 1) & (index_plane != 1)
    inverse = jnp.where(odd_plane[None, :], -jnp.sin(angles), jnp.cos(angles))
    weights = jnp.where(index_plane == 0, 1.0, 2.0).astype(jnp.float32) / quad_points
    forward = weights[:, None] * inverse.T
    return (inverse.astype(jnp.bfloat16), forward.astype(jnp.bfloat16))


def lamb_vector(velocity_phys, vorticity_phys):
    first = velocity_phys[1] * vorticity_phys[2] - velocity_phys[2] * vorticity_phys[1]
    second = velocity_phys[2] * vorticity_phys[0] - velocity_phys[0] * vorticity_phys[2]
    third = velocity_phys[0] * vorticity_phys[1] - velocity_phys[1] * vorticity_phys[0]
    return jnp.stack([first, second, third])


def chain_kernel(position_ref, *refs, group_size):
    group_refs = refs[:group_size]
    sides_ref, out_ref = refs[group_size:]
    slab_count = sides_ref.shape[0]

    def apply(matrix, vectors):
        return lax.dot_general(
            vectors,
            matrix,
            (((1,), (1,)), ((), ())),
            precision=HIGHEST,
            preferred_element_type=jnp.float32,
        )

    def solve(position):
        def blocks_of(slab):
            group_slot = (slab % group_size - position) % group_size
            spot_slot = (slab // group_size - position) % group_size
            return group_refs[group_slot].at[spot_slot]

        zero = jnp.zeros(sides_ref.shape[2:], jnp.float32)
        forward_values = [zero]
        for k in range(1, slab_count):
            source = sides_ref[k, 0] + sides_ref[k - 1, 1]
            forward_values.append(source - apply(blocks_of(k)[0], forward_values[-1]))
        after = zero
        for k in range(slab_count - 1, 0, -1):
            blocks = blocks_of(k)
            solved = apply(blocks[2], forward_values[k]) - apply(blocks[1], after)
            out_ref[k, 0] = solved
            out_ref[k, 1] = after
            after = solved
        out_ref[0, 0] = zero
        out_ref[0, 1] = after

    for position in range(group_size):
        pl.when(position_ref[0] == position)(functools.partial(solve, position))


def on_device(
    velocity,
    vorticity,
    lift,
    extend,
    interface_chain_factors,
    pivot_inverse,
    interior_diag,
    node_map,
    *,
    slab_count,
):
    components, planes_dev, line_count, point_total = velocity.shape
    quad_points = 3 * PLANES // 2
    slab_index = lax.axis_index("slab")
    group_size = planes_dev
    group_count = slab_count // group_size
    position = slab_index // group_size
    owners = [plane * group_size + plane for plane in range(planes_dev)]

    blocks = jnp.stack(
        [interface_chain_factors[0], interface_chain_factors[1], pivot_inverse], axis=1
    )
    within = [blocks[position]]
    for offset in range(1, group_count):
        pairs = [
            (rest + group_size * rank, rest + group_size * ((rank - offset) % group_count))
            for rest in range(group_size)
            for rank in range(group_count)
        ]
        within.append(lax.ppermute(blocks[(position - offset) % group_count], "slab", pairs))
    group_blocks = jnp.stack(within)

    halfway_offsets = jnp.concatenate(
        [jnp.zeros((point_total,), jnp.int32), jnp.full((point_total,), point_total, jnp.int32)]
    )
    row_order = node_map[0] + halfway_offsets
    one_hot = (
        row_order[:, None] == jnp.arange(2 * point_total, dtype=jnp.int32)[None, :]
    ).astype(jnp.bfloat16)
    lift_rows = jnp.einsum(
        "ir,rf->if", one_hot, lift, preferred_element_type=jnp.float32
    ).astype(jnp.bfloat16)
    extend_cols = jnp.einsum(
        "hr,ir->hi", extend, one_hot, preferred_element_type=jnp.float32
    ).astype(jnp.bfloat16)

    inverse, forward = spectral_tables(PLANES, quad_points)
    wavenum = lax.dynamic_slice_in_dim(
        plane_numbers(PLANES), lax.axis_index("mode") * planes_dev, planes_dev
    )
    shifts = plane_shift(wavenum)
    velocity_half = velocity.astype(jnp.bfloat16)
    both_fields = jnp.concatenate([velocity_half, vorticity], axis=0)
    field_lines = lax.all_to_all(both_fields, "mode", split_axis=2, concat_axis=1, tiled=True)
    group_blocks, field_lines = lax.optimization_barrier((group_blocks, field_lines))
    across = [group_blocks]
    for offset in range(1, group_size):
        pairs = [
            (plane * group_size + (plane + offset) % group_size, owners[plane])
            for plane in range(planes_dev)
        ]
        across.append(lax.ppermute(group_blocks, "slab", pairs))
    phys = jnp.einsum("qp,cplb->cqlb", inverse, field_lines, preferred_element_type=jnp.float32)
    lamb_field = lamb_vector(phys[:components], phys[components:]).astype(jnp.bfloat16)
    nonlin_lines = jnp.einsum(
        "pq,cqlb->cplb", forward, lamb_field, preferred_element_type=jnp.float32
    ).astype(jnp.bfloat16)
    interior_point_velocity = (
        (LAMBDA_TIMESTEP * velocity[:, :, 1:, :])
        .astype(jnp.bfloat16)
        .reshape(components, planes_dev, -1)
    )
    lifted_velocity = jnp.einsum(
        "hf,vqf->qvh", lift_rows, interior_point_velocity, preferred_element_type=jnp.float32
    )
    nonlin = lax.all_to_all(nonlin_lines, "mode", split_axis=1, concat_axis=2, tiled=True)
    inner_nonlinear_term = nonlin[:, :, 1:, :].reshape(components, planes_dev, -1)
    cond_line = lifted_velocity + jnp.einsum(
        "hf,vqf->qvh", lift_rows, inner_nonlinear_term, preferred_element_type=jnp.float32
    )
    line_zero_rhs = jnp.swapaxes(
        LAMBDA_TIMESTEP * velocity[:, :, 0, :] + nonlin[:, :, 0, :].astype(jnp.float32), 0, 1
    )
    rhs_left = cond_line[:, :, :point_total] + line_zero_rhs
    right_part = cond_line[:, :, point_total:]

    sides = jnp.stack([rhs_left, right_part], axis=1)
    destination_plane = jnp.asarray(
        [owners.index(slab) if slab in owners else 0 for slab in range(slab_count)], jnp.int32
    )
    to_owner = lax.all_to_all(
        sides[destination_plane], "slab", split_axis=0, concat_axis=0, tiled=True
    )
    both_sides = pl.pallas_call(
        functools.partial(chain_kernel, group_size=group_size),
        out_shape=jax.ShapeDtypeStruct(to_owner.shape, jnp.float32),
        in_specs=[pl.BlockSpec(memory_space=pltpu.SMEM)]
        + [pl.BlockSpec(memory_space=pltpu.VMEM)] * (group_size + 1),
        out_specs=pl.BlockSpec(memory_space=pltpu.VMEM),
    )(position.astype(jnp.int32).reshape(1), *across, to_owner)
    from_owner = lax.all_to_all(both_sides, "slab", split_axis=0, concat_axis=0, tiled=True)
    mine = from_owner[jnp.asarray(owners)]
    left_values = mine[:, 0]
    right_values = mine[:, 1]

    boundary_line = jnp.concatenate([left_values, right_values], axis=2).astype(jnp.bfloat16)
    extension = jnp.einsum(
        "hg,dog->odh", extend_cols, boundary_line, preferred_element_type=jnp.float32
    )
    extension = extension.reshape(components, planes_dev, line_count - 1, point_total)
    inner_rhs = LAMBDA_TIMESTEP * velocity[:, :, 1:, :] + nonlin[:, :, 1:, :].astype(jnp.float32)
    new_inner = extension + inner_rhs / (interior_diag[None, None] + shifts[None, :, None, None])
    line_zero = jnp.swapaxes(left_values, 0, 1)
    return jnp.concatenate([line_zero[:, :, None, :], new_inner], axis=2)


def solution(mesh):
    in_specs = (
        P(None, "mode", "slab", None),
        P(None, "mode", "slab", None),
        P("slab", None),
        P("slab", None),
        P(None, "mode", "slab", None),
        P("mode", "slab", None),
        P("slab", None),
        P("slab", None),
    )
    out_specs = P(None, "mode", "slab", None)
    return jax.shard_map(
        functools.partial(on_device, slab_count=mesh.shape["slab"]), mesh=mesh, in_specs=in_specs, out_specs=out_specs, check_vma=False
    )
```

```python
import functools

import jax
import jax.numpy as jnp
from jax import lax
from jax.experimental import pallas as pl
from jax.experimental.pallas import tpu as pltpu
from jax.sharding import PartitionSpec as P

PLANES = 64


LAMBDA_TIMESTEP = 0.5
WAVE_BASE = 0.125
HIGHEST = lax.Precision.HIGHEST


def plane_numbers(planes):
    index_plane = jnp.arange(planes, dtype=jnp.int32)
    return jnp.where(index_plane == 1, planes // 2, index_plane // 2)


def plane_shift(wavenum):
    return LAMBDA_TIMESTEP + (wavenum.astype(jnp.float32) * WAVE_BASE) ** 2


def spectral_tables(planes, quad_points):
    wavenum = plane_numbers(planes)
    station = jnp.arange(quad_points, dtype=jnp.int32)
    phases = station[:, None] * wavenum[None, :] % quad_points
    angles = phases.astype(jnp.float32) * (2.0 * jnp.pi / quad_points)
    index_plane = jnp.arange(planes, dtype=jnp.int32)
    odd_plane = (index_plane % 2 == 1) & (index_plane != 1)
    inverse = jnp.where(odd_plane[None, :], -jnp.sin(angles), jnp.cos(angles))
    weights = jnp.where(index_plane == 0, 1.0, 2.0).astype(jnp.float32) / quad_points
    forward = weights[:, None] * inverse.T
    return (inverse.astype(jnp.bfloat16), forward.astype(jnp.bfloat16))


def lamb_vector(velocity_phys, vorticity_phys):
    first = velocity_phys[1] * vorticity_phys[2] - velocity_phys[2] * vorticity_phys[1]
    second = velocity_phys[2] * vorticity_phys[0] - velocity_phys[0] * vorticity_phys[2]
    third = velocity_phys[0] * vorticity_phys[1] - velocity_phys[1] * vorticity_phys[0]
    return jnp.stack([first, second, third])


def chain_kernel(position_ref, *refs, group_size):
    group_refs = refs[:group_size]
    sides_ref, out_ref = refs[group_size:]
    slab_count = sides_ref.shape[0]

    def apply(matrix, vectors):
        return lax.dot_general(
            vectors,
            matrix,
            (((1,), (1,)), ((), ())),
            precision=lax.Precision.HIGH,
            preferred_element_type=jnp.float32,
        )

    def solve(position):
        def blocks_of(slab):
            group_slot = (slab % group_size - position) % group_size
            spot_slot = (slab // group_size - position) % group_size
            return group_refs[group_slot].at[spot_slot]

        zero = jnp.zeros(sides_ref.shape[2:], jnp.float32)
        forward_values = [zero]
        for k in range(1, slab_count):
            source = sides_ref[k, 0] + sides_ref[k - 1, 1]
            forward_values.append(source - apply(blocks_of(k)[0], forward_values[-1]))
        after = zero
        for k in range(slab_count - 1, 0, -1):
            blocks = blocks_of(k)
            solved = apply(blocks[2], forward_values[k]) - apply(blocks[1], after)
            out_ref[k, 0] = solved
            out_ref[k, 1] = after
            after = solved
        out_ref[0, 0] = zero
        out_ref[0, 1] = after

    for position in range(group_size):
        pl.when(position_ref[0] == position)(functools.partial(solve, position))


def on_device(
    velocity,
    vorticity,
    lift,
    extend,
    interface_chain_factors,
    pivot_inverse,
    interior_diag,
    node_map,
    *,
    slab_count,
):
    components, planes_dev, line_count, point_total = velocity.shape
    quad_points = 3 * PLANES // 2
    slab_index = lax.axis_index("slab")
    group_size = planes_dev
    group_count = slab_count // group_size
    position = slab_index // group_size
    owners = [plane * group_size + plane for plane in range(planes_dev)]

    blocks = jnp.stack(
        [interface_chain_factors[0], interface_chain_factors[1], pivot_inverse], axis=1
    )
    within = [blocks[position]]
    for offset in range(1, group_count):
        pairs = [
            (rest + group_size * rank, rest + group_size * ((rank - offset) % group_count))
            for rest in range(group_size)
            for rank in range(group_count)
        ]
        within.append(lax.ppermute(blocks[(position - offset) % group_count], "slab", pairs))
    group_blocks = jnp.stack(within)

    halfway_offsets = jnp.concatenate(
        [jnp.zeros((point_total,), jnp.int32), jnp.full((point_total,), point_total, jnp.int32)]
    )
    row_order = node_map[0] + halfway_offsets
    one_hot = (
        row_order[:, None] == jnp.arange(2 * point_total, dtype=jnp.int32)[None, :]
    ).astype(jnp.bfloat16)
    lift_rows = jnp.einsum(
        "ir,rf->if", one_hot, lift, preferred_element_type=jnp.float32
    ).astype(jnp.bfloat16)
    extend_cols = jnp.einsum(
        "hr,ir->hi", extend, one_hot, preferred_element_type=jnp.float32
    ).astype(jnp.bfloat16)

    inverse, forward = spectral_tables(PLANES, quad_points)
    wavenum = lax.dynamic_slice_in_dim(
        plane_numbers(PLANES), lax.axis_index("mode") * planes_dev, planes_dev
    )
    shifts = plane_shift(wavenum)
    velocity_half = velocity.astype(jnp.bfloat16)
    both_fields = jnp.concatenate([velocity_half, vorticity], axis=0)
    field_lines = lax.all_to_all(both_fields, "mode", split_axis=2, concat_axis=1, tiled=True)
    group_blocks, field_lines = lax.optimization_barrier((group_blocks, field_lines))
    across = [group_blocks]
    for offset in range(1, group_size):
        pairs = [
            (plane * group_size + (plane + offset) % group_size, owners[plane])
            for plane in range(planes_dev)
        ]
        across.append(lax.ppermute(group_blocks, "slab", pairs))
    phys = jnp.einsum("qp,cplb->cqlb", inverse, field_lines, preferred_element_type=jnp.float32)
    lamb_field = lamb_vector(phys[:components], phys[components:]).astype(jnp.bfloat16)
    nonlin_lines = jnp.einsum(
        "pq,cqlb->cplb", forward, lamb_field, preferred_element_type=jnp.float32
    ).astype(jnp.bfloat16)
    interior_point_velocity = (
        (LAMBDA_TIMESTEP * velocity[:, :, 1:, :])
        .astype(jnp.bfloat16)
        .reshape(components, planes_dev, -1)
    )
    lifted_velocity = jnp.einsum(
        "hf,vqf->qvh", lift_rows, interior_point_velocity, preferred_element_type=jnp.float32
    )
    nonlin = lax.all_to_all(nonlin_lines, "mode", split_axis=1, concat_axis=2, tiled=True)
    inner_nonlinear_term = nonlin[:, :, 1:, :].reshape(components, planes_dev, -1)
    cond_line = lifted_velocity + jnp.einsum(
        "hf,vqf->qvh", lift_rows, inner_nonlinear_term, preferred_element_type=jnp.float32
    )
    line_zero_rhs = jnp.swapaxes(
        LAMBDA_TIMESTEP * velocity[:, :, 0, :] + nonlin[:, :, 0, :].astype(jnp.float32), 0, 1
    )
    rhs_left = cond_line[:, :, :point_total] + line_zero_rhs
    right_part = cond_line[:, :, point_total:]

    sides = jnp.stack([rhs_left, right_part], axis=1)
    destination_plane = [owners.index(slab) if slab in owners else 0 for slab in range(slab_count)]
    outgoing = jnp.stack([sides[plane] for plane in destination_plane])
    to_owner = lax.all_to_all(outgoing, "slab", split_axis=0, concat_axis=0, tiled=True)
    both_sides = pl.pallas_call(
        functools.partial(chain_kernel, group_size=group_size),
        out_shape=jax.ShapeDtypeStruct(to_owner.shape, jnp.float32),
        in_specs=[pl.BlockSpec(memory_space=pltpu.SMEM)]
        + [pl.BlockSpec(memory_space=pltpu.VMEM)] * (group_size + 1),
        out_specs=pl.BlockSpec(memory_space=pltpu.VMEM),
    )(position.astype(jnp.int32).reshape(1), *across, to_owner)
    from_owner = lax.all_to_all(both_sides, "slab", split_axis=0, concat_axis=0, tiled=True)
    mine = jnp.stack([from_owner[owner] for owner in owners])
    left_values = mine[:, 0]
    right_values = mine[:, 1]

    boundary_line = jnp.concatenate([left_values, right_values], axis=2).astype(jnp.bfloat16)
    extension = jnp.einsum(
        "hg,dog->odh", extend_cols, boundary_line, preferred_element_type=jnp.float32
    )
    extension = extension.reshape(components, planes_dev, line_count - 1, point_total)
    inner_rhs = LAMBDA_TIMESTEP * velocity[:, :, 1:, :] + nonlin[:, :, 1:, :].astype(jnp.float32)
    new_inner = extension + inner_rhs / (interior_diag[None, None] + shifts[None, :, None, None])
    line_zero = jnp.swapaxes(left_values, 0, 1)
    return jnp.concatenate([line_zero[:, :, None, :], new_inner], axis=2)


def solution(mesh):
    in_specs = (
        P(None, "mode", "slab", None),
        P(None, "mode", "slab", None),
        P("slab", None),
        P("slab", None),
        P(None, "mode", "slab", None),
        P("mode", "slab", None),
        P("slab", None),
        P("slab", None),
    )
    out_specs = P(None, "mode", "slab", None)
    return jax.shard_map(
        functools.partial(on_device, slab_count=mesh.shape["slab"]), mesh=mesh, in_specs=in_specs, out_specs=out_specs, check_vma=False
    )
```

```python
import functools

import jax
import jax.numpy as jnp
from jax import lax
from jax.experimental import pallas as pl
from jax.experimental.pallas import tpu as pltpu
from jax.sharding import PartitionSpec as P

PLANES = 64


LAMBDA_TIMESTEP = 0.5
WAVE_BASE = 0.125
HIGHEST = lax.Precision.HIGHEST


def plane_numbers(planes):
    index_plane = jnp.arange(planes, dtype=jnp.int32)
    return jnp.where(index_plane == 1, planes // 2, index_plane // 2)


def plane_shift(wavenum):
    return LAMBDA_TIMESTEP + (wavenum.astype(jnp.float32) * WAVE_BASE) ** 2


def spectral_tables(planes, quad_points):
    wavenum = plane_numbers(planes)
    station = jnp.arange(quad_points, dtype=jnp.int32)
    phases = station[:, None] * wavenum[None, :] % quad_points
    angles = phases.astype(jnp.float32) * (2.0 * jnp.pi / quad_points)
    index_plane = jnp.arange(planes, dtype=jnp.int32)
    odd_plane = (index_plane % 2 == 1) & (index_plane != 1)
    inverse = jnp.where(odd_plane[None, :], -jnp.sin(angles), jnp.cos(angles))
    weights = jnp.where(index_plane == 0, 1.0, 2.0).astype(jnp.float32) / quad_points
    forward = weights[:, None] * inverse.T
    return (inverse.astype(jnp.bfloat16), forward.astype(jnp.bfloat16))


def lamb_vector(velocity_phys, vorticity_phys):
    first = velocity_phys[1] * vorticity_phys[2] - velocity_phys[2] * vorticity_phys[1]
    second = velocity_phys[2] * vorticity_phys[0] - velocity_phys[0] * vorticity_phys[2]
    third = velocity_phys[0] * vorticity_phys[1] - velocity_phys[1] * vorticity_phys[0]
    return jnp.stack([first, second, third])


def chain_kernel(position_ref, *refs, group_size):
    group_refs = refs[:group_size]
    sides_ref, out_ref = refs[group_size:]
    slab_count = sides_ref.shape[0]

    def apply(matrix, vectors):
        return lax.dot_general(
            vectors,
            matrix,
            (((1,), (1,)), ((), ())),
            precision=lax.Precision.HIGH,
            preferred_element_type=jnp.float32,
        )

    def solve(position):
        def blocks_of(slab):
            label = (slab + 1) % slab_count
            group_slot = (label % group_size - 1) % group_size
            spot_slot = (label // group_size - position) % group_size
            return group_refs[group_slot].at[spot_slot]

        zero = jnp.zeros(sides_ref.shape[2:], jnp.float32)
        forward_values = [zero]
        for k in range(1, slab_count):
            source = sides_ref[k, 0] + sides_ref[k - 1, 1]
            forward_values.append(source - apply(blocks_of(k)[0], forward_values[-1]))
        after = zero
        for k in range(slab_count - 1, 0, -1):
            blocks = blocks_of(k)
            solved = apply(blocks[2], forward_values[k]) - apply(blocks[1], after)
            out_ref[k, 0] = solved
            out_ref[k, 1] = after
            after = solved
        out_ref[0, 0] = zero
        out_ref[0, 1] = after

    for position in range(group_size):
        pl.when(position_ref[0] == position)(functools.partial(solve, position))


def on_device(
    velocity,
    vorticity,
    lift,
    extend,
    interface_chain_factors,
    pivot_inverse,
    interior_diag,
    node_map,
    *,
    slab_count,
):
    components, planes_dev, line_count, point_total = velocity.shape
    quad_points = 3 * PLANES // 2
    slab_index = lax.axis_index("slab")
    group_size = planes_dev
    group_count = slab_count // group_size
    position = ((slab_index + 1) % slab_count) // group_size

    def slab_of(label):
        return (label - 1) % slab_count

    owners = [slab_of(plane * group_size + 1) for plane in range(planes_dev)]

    blocks = jnp.stack(
        [interface_chain_factors[0], interface_chain_factors[1], pivot_inverse], axis=1
    )
    within = [blocks[position]]
    for offset in range(1, group_count):
        pairs = [
            (
                slab_of(rest + group_size * rank),
                slab_of(rest + group_size * ((rank - offset) % group_count)),
            )
            for rest in range(group_size)
            for rank in range(group_count)
        ]
        within.append(lax.ppermute(blocks[(position - offset) % group_count], "slab", pairs))
    group_blocks = jnp.stack(within)

    halfway_offsets = jnp.concatenate(
        [jnp.zeros((point_total,), jnp.int32), jnp.full((point_total,), point_total, jnp.int32)]
    )
    row_order = node_map[0] + halfway_offsets
    one_hot = (
        row_order[:, None] == jnp.arange(2 * point_total, dtype=jnp.int32)[None, :]
    ).astype(jnp.bfloat16)
    lift_rows = jnp.einsum(
        "ir,rf->if", one_hot, lift, preferred_element_type=jnp.float32
    ).astype(jnp.bfloat16)
    extend_cols = jnp.einsum(
        "hr,ir->hi", extend, one_hot, preferred_element_type=jnp.float32
    ).astype(jnp.bfloat16)

    inverse, forward = spectral_tables(PLANES, quad_points)
    wavenum = lax.dynamic_slice_in_dim(
        plane_numbers(PLANES), lax.axis_index("mode") * planes_dev, planes_dev
    )
    shifts = plane_shift(wavenum)
    velocity_half = velocity.astype(jnp.bfloat16)
    both_fields = jnp.concatenate([velocity_half, vorticity], axis=0)
    field_lines = lax.all_to_all(both_fields, "mode", split_axis=2, concat_axis=1, tiled=True)
    group_blocks, field_lines = lax.optimization_barrier((group_blocks, field_lines))
    across = [group_blocks]
    for offset in range(1, group_size):
        pairs = [
            (slab_of(plane * group_size + (1 + offset) % group_size), owners[plane])
            for plane in range(planes_dev)
        ]
        across.append(lax.ppermute(group_blocks, "slab", pairs))
    phys = jnp.einsum("qp,cplb->cqlb", inverse, field_lines, preferred_element_type=jnp.float32)
    lamb_field = lamb_vector(phys[:components], phys[components:]).astype(jnp.bfloat16)
    nonlin_lines = jnp.einsum(
        "pq,cqlb->cplb", forward, lamb_field, preferred_element_type=jnp.float32
    ).astype(jnp.bfloat16)
    interior_point_velocity = (
        (LAMBDA_TIMESTEP * velocity[:, :, 1:, :])
        .astype(jnp.bfloat16)
        .reshape(components, planes_dev, -1)
    )
    lifted_velocity = jnp.einsum(
        "hf,vqf->qvh", lift_rows, interior_point_velocity, preferred_element_type=jnp.float32
    )
    nonlin = lax.all_to_all(nonlin_lines, "mode", split_axis=1, concat_axis=2, tiled=True)
    inner_nonlinear_term = nonlin[:, :, 1:, :].reshape(components, planes_dev, -1)
    cond_line = lifted_velocity + jnp.einsum(
        "hf,vqf->qvh", lift_rows, inner_nonlinear_term, preferred_element_type=jnp.float32
    )
    line_zero_rhs = jnp.swapaxes(
        LAMBDA_TIMESTEP * velocity[:, :, 0, :] + nonlin[:, :, 0, :].astype(jnp.float32), 0, 1
    )
    rhs_left = cond_line[:, :, :point_total] + line_zero_rhs
    right_part = cond_line[:, :, point_total:]

    sides = jnp.stack([rhs_left, right_part], axis=1)
    destination_plane = [owners.index(slab) if slab in owners else 0 for slab in range(slab_count)]
    outgoing = jnp.stack([sides[plane] for plane in destination_plane])
    to_owner = lax.all_to_all(outgoing, "slab", split_axis=0, concat_axis=0, tiled=True)
    both_sides = pl.pallas_call(
        functools.partial(chain_kernel, group_size=group_size),
        out_shape=jax.ShapeDtypeStruct(to_owner.shape, jnp.float32),
        in_specs=[pl.BlockSpec(memory_space=pltpu.SMEM)]
        + [pl.BlockSpec(memory_space=pltpu.VMEM)] * (group_size + 1),
        out_specs=pl.BlockSpec(memory_space=pltpu.VMEM),
    )(position.astype(jnp.int32).reshape(1), *across, to_owner)
    from_owner = lax.all_to_all(both_sides, "slab", split_axis=0, concat_axis=0, tiled=True)
    mine = jnp.stack([from_owner[owner] for owner in owners])
    left_values = mine[:, 0]
    right_values = mine[:, 1]

    boundary_line = jnp.concatenate([left_values, right_values], axis=2).astype(jnp.bfloat16)
    extension = jnp.einsum(
        "hg,dog->odh", extend_cols, boundary_line, preferred_element_type=jnp.float32
    )
    extension = extension.reshape(components, planes_dev, line_count - 1, point_total)
    inner_rhs = LAMBDA_TIMESTEP * velocity[:, :, 1:, :] + nonlin[:, :, 1:, :].astype(jnp.float32)
    new_inner = extension + inner_rhs / (interior_diag[None, None] + shifts[None, :, None, None])
    line_zero = jnp.swapaxes(left_values, 0, 1)
    return jnp.concatenate([line_zero[:, :, None, :], new_inner], axis=2)


def solution(mesh):
    in_specs = (
        P(None, "mode", "slab", None),
        P(None, "mode", "slab", None),
        P("slab", None),
        P("slab", None),
        P(None, "mode", "slab", None),
        P("mode", "slab", None),
        P("slab", None),
        P("slab", None),
    )
    out_specs = P(None, "mode", "slab", None)
    return jax.shard_map(
        functools.partial(on_device, slab_count=mesh.shape["slab"]), mesh=mesh, in_specs=in_specs, out_specs=out_specs, check_vma=False
    )
```

```python
import functools

import jax
import jax.numpy as jnp
from jax import lax
from jax.experimental import pallas as pl
from jax.experimental.pallas import tpu as pltpu
from jax.sharding import PartitionSpec as P

PLANES = 64


LAMBDA_TIMESTEP = 0.5
WAVE_BASE = 0.125
HIGHEST = lax.Precision.HIGHEST


def plane_numbers(planes):
    index_plane = jnp.arange(planes, dtype=jnp.int32)
    return jnp.where(index_plane == 1, planes // 2, index_plane // 2)


def plane_shift(wavenum):
    return LAMBDA_TIMESTEP + (wavenum.astype(jnp.float32) * WAVE_BASE) ** 2


def spectral_tables(planes, quad_points):
    wavenum = plane_numbers(planes)
    station = jnp.arange(quad_points, dtype=jnp.int32)
    phases = station[:, None] * wavenum[None, :] % quad_points
    angles = phases.astype(jnp.float32) * (2.0 * jnp.pi / quad_points)
    index_plane = jnp.arange(planes, dtype=jnp.int32)
    odd_plane = (index_plane % 2 == 1) & (index_plane != 1)
    inverse = jnp.where(odd_plane[None, :], -jnp.sin(angles), jnp.cos(angles))
    weights = jnp.where(index_plane == 0, 1.0, 2.0).astype(jnp.float32) / quad_points
    forward = weights[:, None] * inverse.T
    return (inverse.astype(jnp.bfloat16), forward.astype(jnp.bfloat16))


def lamb_vector(velocity_phys, vorticity_phys):
    first = velocity_phys[1] * vorticity_phys[2] - velocity_phys[2] * vorticity_phys[1]
    second = velocity_phys[2] * vorticity_phys[0] - velocity_phys[0] * vorticity_phys[2]
    third = velocity_phys[0] * vorticity_phys[1] - velocity_phys[1] * vorticity_phys[0]
    return jnp.stack([first, second, third])


def chain_kernel(position_ref, *refs, group_size):
    group_refs = refs[:group_size]
    sides_ref, out_ref = refs[group_size:]
    slab_count = sides_ref.shape[0]

    def apply(matrix, vectors):
        return lax.dot_general(
            vectors,
            matrix,
            (((1,), (1,)), ((), ())),
            precision=lax.Precision.HIGH,
            preferred_element_type=jnp.float32,
        )

    def solve(position):
        def blocks_of(slab):
            label = (slab + 1) % slab_count
            group_slot = (label % group_size - 1) % group_size
            spot_slot = (label // group_size - position) % group_size
            return group_refs[group_slot].at[spot_slot]

        zero = jnp.zeros((sides_ref.shape[1], sides_ref.shape[3]), jnp.float32)
        sides = [sides_ref[k] for k in range(slab_count)]
        forward_values = [zero]
        for k in range(1, slab_count):
            source = sides[k][:, 0] + sides[k - 1][:, 1]
            forward_values.append(source - apply(blocks_of(k)[0], forward_values[-1]))
        after = zero
        for k in range(slab_count - 1, 0, -1):
            blocks = blocks_of(k)
            solved = apply(blocks[2], forward_values[k]) - apply(blocks[1], after)
            out_ref[k] = jnp.stack([solved, after], axis=1)
            after = solved
        out_ref[0] = jnp.stack([zero, after], axis=1)

    for position in range(group_size):
        pl.when(position_ref[0] == position)(functools.partial(solve, position))


def on_device(
    velocity,
    vorticity,
    lift,
    extend,
    interface_chain_factors,
    pivot_inverse,
    interior_diag,
    node_map,
    *,
    slab_count,
):
    components, planes_dev, line_count, point_total = velocity.shape
    quad_points = 3 * PLANES // 2
    slab_index = lax.axis_index("slab")
    group_size = planes_dev
    group_count = slab_count // group_size
    position = ((slab_index + 1) % slab_count) // group_size

    def slab_of(label):
        return (label - 1) % slab_count

    owners = [slab_of(plane * group_size + 1) for plane in range(planes_dev)]

    blocks = jnp.stack(
        [interface_chain_factors[0], interface_chain_factors[1], pivot_inverse], axis=1
    )
    within = [blocks[position]]
    for offset in range(1, group_count):
        pairs = [
            (
                slab_of(rest + group_size * rank),
                slab_of(rest + group_size * ((rank - offset) % group_count)),
            )
            for rest in range(group_size)
            for rank in range(group_count)
        ]
        within.append(lax.ppermute(blocks[(position - offset) % group_count], "slab", pairs))
    group_blocks = jnp.stack(within)

    halfway_offsets = jnp.concatenate(
        [jnp.zeros((point_total,), jnp.int32), jnp.full((point_total,), point_total, jnp.int32)]
    )
    row_order = node_map[0] + halfway_offsets
    one_hot = (
        row_order[:, None] == jnp.arange(2 * point_total, dtype=jnp.int32)[None, :]
    ).astype(jnp.bfloat16)
    lift_rows = jnp.einsum(
        "ir,rf->if", one_hot, lift, preferred_element_type=jnp.float32
    ).astype(jnp.bfloat16)
    extend_cols = jnp.einsum(
        "hr,ir->hi", extend, one_hot, preferred_element_type=jnp.float32
    ).astype(jnp.bfloat16)

    inverse, forward = spectral_tables(PLANES, quad_points)
    wavenum = lax.dynamic_slice_in_dim(
        plane_numbers(PLANES), lax.axis_index("mode") * planes_dev, planes_dev
    )
    shifts = plane_shift(wavenum)
    velocity_half = velocity.astype(jnp.bfloat16)
    both_fields = jnp.concatenate([velocity_half, vorticity], axis=0)
    field_lines = lax.all_to_all(both_fields, "mode", split_axis=2, concat_axis=1, tiled=True)
    group_blocks, field_lines = lax.optimization_barrier((group_blocks, field_lines))
    across = [group_blocks]
    for offset in range(1, group_size):
        pairs = [
            (slab_of(plane * group_size + (1 + offset) % group_size), owners[plane])
            for plane in range(planes_dev)
        ]
        across.append(lax.ppermute(group_blocks, "slab", pairs))
    phys = jnp.einsum("qp,cplb->cqlb", inverse, field_lines, preferred_element_type=jnp.float32)
    lamb_field = lamb_vector(phys[:components], phys[components:]).astype(jnp.bfloat16)
    nonlin_lines = jnp.einsum(
        "pq,cqlb->cplb", forward, lamb_field, preferred_element_type=jnp.float32
    ).astype(jnp.bfloat16)
    interior_point_velocity = (
        (LAMBDA_TIMESTEP * velocity[:, :, 1:, :])
        .astype(jnp.bfloat16)
        .reshape(components, planes_dev, -1)
    )
    lifted_velocity = jnp.einsum(
        "hf,vqf->qvh", lift_rows, interior_point_velocity, preferred_element_type=jnp.float32
    )
    nonlin = lax.all_to_all(nonlin_lines, "mode", split_axis=1, concat_axis=2, tiled=True)
    inner_nonlinear_term = nonlin[:, :, 1:, :].reshape(components, planes_dev, -1)
    cond_line = lifted_velocity + jnp.einsum(
        "hf,vqf->qvh", lift_rows, inner_nonlinear_term, preferred_element_type=jnp.float32
    )
    line_zero_rhs = jnp.swapaxes(
        LAMBDA_TIMESTEP * velocity[:, :, 0, :] + nonlin[:, :, 0, :].astype(jnp.float32), 0, 1
    )
    rhs_left = cond_line[:, :, :point_total] + line_zero_rhs
    right_part = cond_line[:, :, point_total:]

    sides = jnp.stack([rhs_left, right_part], axis=2)
    destination_plane = [owners.index(slab) if slab in owners else 0 for slab in range(slab_count)]
    outgoing = jnp.stack([sides[plane] for plane in destination_plane])
    to_owner = lax.all_to_all(outgoing, "slab", split_axis=0, concat_axis=0, tiled=True)
    both_sides = pl.pallas_call(
        functools.partial(chain_kernel, group_size=group_size),
        out_shape=jax.ShapeDtypeStruct(to_owner.shape, jnp.float32),
        in_specs=[pl.BlockSpec(memory_space=pltpu.SMEM)]
        + [pl.BlockSpec(memory_space=pltpu.VMEM)] * (group_size + 1),
        out_specs=pl.BlockSpec(memory_space=pltpu.VMEM),
    )(position.astype(jnp.int32).reshape(1), *across, to_owner)
    from_owner = lax.all_to_all(both_sides, "slab", split_axis=0, concat_axis=0, tiled=True)
    mine = jnp.stack([from_owner[owner] for owner in owners])
    left_values = mine[:, :, 0]
    right_values = mine[:, :, 1]

    boundary_line = jnp.concatenate([left_values, right_values], axis=2).astype(jnp.bfloat16)
    extension = jnp.einsum(
        "hg,dog->odh", extend_cols, boundary_line, preferred_element_type=jnp.float32
    )
    extension = extension.reshape(components, planes_dev, line_count - 1, point_total)
    inner_rhs = LAMBDA_TIMESTEP * velocity[:, :, 1:, :] + nonlin[:, :, 1:, :].astype(jnp.float32)
    new_inner = extension + inner_rhs / (interior_diag[None, None] + shifts[None, :, None, None])
    line_zero = jnp.swapaxes(left_values, 0, 1)
    return jnp.concatenate([line_zero[:, :, None, :], new_inner], axis=2)


def solution(mesh):
    in_specs = (
        P(None, "mode", "slab", None),
        P(None, "mode", "slab", None),
        P("slab", None),
        P("slab", None),
        P(None, "mode", "slab", None),
        P("mode", "slab", None),
        P("slab", None),
        P("slab", None),
    )
    out_specs = P(None, "mode", "slab", None)
    return jax.shard_map(
        functools.partial(on_device, slab_count=mesh.shape["slab"]), mesh=mesh, in_specs=in_specs, out_specs=out_specs, check_vma=False
    )
```

```python
import functools

import jax
import jax.numpy as jnp
from jax import lax
from jax.experimental import pallas as pl
from jax.experimental.pallas import tpu as pltpu
from jax.sharding import PartitionSpec as P

PLANES = 64


LAMBDA_TIMESTEP = 0.5
WAVE_BASE = 0.125
HIGHEST = lax.Precision.HIGHEST


def plane_numbers(planes):
    index_plane = jnp.arange(planes, dtype=jnp.int32)
    return jnp.where(index_plane == 1, planes // 2, index_plane // 2)


def plane_shift(wavenum):
    return LAMBDA_TIMESTEP + (wavenum.astype(jnp.float32) * WAVE_BASE) ** 2


def spectral_tables(planes, quad_points):
    wavenum = plane_numbers(planes)
    station = jnp.arange(quad_points, dtype=jnp.int32)
    phases = station[:, None] * wavenum[None, :] % quad_points
    angles = phases.astype(jnp.float32) * (2.0 * jnp.pi / quad_points)
    index_plane = jnp.arange(planes, dtype=jnp.int32)
    odd_plane = (index_plane % 2 == 1) & (index_plane != 1)
    inverse = jnp.where(odd_plane[None, :], -jnp.sin(angles), jnp.cos(angles))
    weights = jnp.where(index_plane == 0, 1.0, 2.0).astype(jnp.float32) / quad_points
    forward = weights[:, None] * inverse.T
    return (inverse.astype(jnp.bfloat16), forward.astype(jnp.bfloat16))


def lamb_vector(velocity_phys, vorticity_phys):
    first = velocity_phys[1] * vorticity_phys[2] - velocity_phys[2] * vorticity_phys[1]
    second = velocity_phys[2] * vorticity_phys[0] - velocity_phys[0] * vorticity_phys[2]
    third = velocity_phys[0] * vorticity_phys[1] - velocity_phys[1] * vorticity_phys[0]
    return jnp.stack([first, second, third])


def chain_kernel(position_ref, *refs, group_size):
    group_refs = refs[:group_size]
    sides_ref, out_ref = refs[group_size:]
    slab_count = sides_ref.shape[0]

    def apply(matrix, vectors):
        return lax.dot_general(
            vectors,
            matrix,
            (((1,), (1,)), ((), ())),
            precision=lax.Precision.HIGH,
            preferred_element_type=jnp.float32,
        )

    def solve(position):
        def blocks_of(slab):
            label = (slab + 1) % slab_count
            group_slot = (label % group_size - 1) % group_size
            spot_slot = (label // group_size - position) % group_size
            return group_refs[group_slot].at[spot_slot]

        zero = jnp.zeros((sides_ref.shape[1], sides_ref.shape[3]), jnp.float32)
        sides = [sides_ref[k] for k in range(slab_count)]
        forward_values = [zero]
        for k in range(1, slab_count):
            source = sides[k][:, 0] + sides[k - 1][:, 1]
            forward_values.append(source - apply(blocks_of(k)[0], forward_values[-1]))
        after = zero
        for k in range(slab_count - 1, 0, -1):
            blocks = blocks_of(k)
            solved = apply(blocks[2], forward_values[k]) - apply(blocks[1], after)
            out_ref[k] = jnp.stack([solved, after], axis=1)
            after = solved
        out_ref[0] = jnp.stack([zero, after], axis=1)

    for position in range(group_size):
        pl.when(position_ref[0] == position)(functools.partial(solve, position))


def on_device(
    velocity,
    vorticity,
    lift,
    extend,
    interface_chain_factors,
    pivot_inverse,
    interior_diag,
    node_map,
    *,
    slab_count,
):
    components, planes_dev, line_count, point_total = velocity.shape
    quad_points = 3 * PLANES // 2
    slab_index = lax.axis_index("slab")
    group_size = planes_dev
    group_count = slab_count // group_size
    position = ((slab_index + 1) % slab_count) // group_size

    def slab_of(label):
        return (label - 1) % slab_count

    owners = [slab_of(plane * group_size + 1) for plane in range(planes_dev)]

    blocks = jnp.stack(
        [interface_chain_factors[0], interface_chain_factors[1], pivot_inverse], axis=1
    )
    within = [blocks[position]]
    for offset in range(1, group_count):
        pairs = [
            (
                slab_of(rest + group_size * rank),
                slab_of(rest + group_size * ((rank - offset) % group_count)),
            )
            for rest in range(group_size)
            for rank in range(group_count)
        ]
        within.append(lax.ppermute(blocks[(position - offset) % group_count], "slab", pairs))
    group_blocks = jnp.stack(within)

    halfway_offsets = jnp.concatenate(
        [jnp.zeros((point_total,), jnp.int32), jnp.full((point_total,), point_total, jnp.int32)]
    )
    row_order = node_map[0] + halfway_offsets
    one_hot = (
        row_order[:, None] == jnp.arange(2 * point_total, dtype=jnp.int32)[None, :]
    ).astype(jnp.bfloat16)
    lift_rows = jnp.einsum(
        "ir,rf->if", one_hot, lift, preferred_element_type=jnp.float32
    ).astype(jnp.bfloat16)
    extend_cols = jnp.einsum(
        "hr,ir->hi", extend, one_hot, preferred_element_type=jnp.float32
    ).astype(jnp.bfloat16)

    inverse, forward = spectral_tables(PLANES, quad_points)
    wavenum = lax.dynamic_slice_in_dim(
        plane_numbers(PLANES), lax.axis_index("mode") * planes_dev, planes_dev
    )
    shifts = plane_shift(wavenum)
    velocity_half = velocity.astype(jnp.bfloat16)
    both_fields = jnp.concatenate([velocity_half, vorticity], axis=0)
    field_lines = lax.all_to_all(both_fields, "mode", split_axis=2, concat_axis=1, tiled=True)
    group_blocks, field_lines = lax.optimization_barrier((group_blocks, field_lines))
    across = [group_blocks]
    for offset in range(1, group_size):
        pairs = [
            (slab_of(plane * group_size + (1 + offset) % group_size), owners[plane])
            for plane in range(planes_dev)
        ]
        across.append(lax.ppermute(group_blocks, "slab", pairs))
    phys = jnp.einsum("qp,cplb->cqlb", inverse, field_lines, preferred_element_type=jnp.float32)
    lamb_field = lamb_vector(phys[:components], phys[components:]).astype(jnp.bfloat16)
    nonlin_lines = jnp.einsum(
        "pq,cqlb->cplb", forward, lamb_field, preferred_element_type=jnp.float32
    ).astype(jnp.bfloat16)
    interior_point_velocity = (
        (LAMBDA_TIMESTEP * velocity[:, :, 1:, :])
        .astype(jnp.bfloat16)
        .reshape(components, planes_dev, -1)
    )
    lifted_velocity = jnp.einsum(
        "hf,vqf->qvh", lift_rows, interior_point_velocity, preferred_element_type=jnp.float32
    )
    nonlin = lax.all_to_all(nonlin_lines, "mode", split_axis=1, concat_axis=2, tiled=True)
    inner_nonlinear_term = nonlin[:, :, 1:, :].reshape(components, planes_dev, -1)
    cond_line = lifted_velocity + jnp.einsum(
        "hf,vqf->qvh", lift_rows, inner_nonlinear_term, preferred_element_type=jnp.float32
    )
    line_zero_rhs = jnp.swapaxes(
        LAMBDA_TIMESTEP * velocity[:, :, 0, :] + nonlin[:, :, 0, :].astype(jnp.float32), 0, 1
    )
    rhs_left = cond_line[:, :, :point_total] + line_zero_rhs
    right_part = cond_line[:, :, point_total:]

    sides = jnp.stack([rhs_left, right_part], axis=2)
    assert all(owner // group_size == plane for plane, owner in enumerate(owners))
    outgoing = jnp.repeat(sides, group_size, axis=0)
    to_owner = lax.all_to_all(outgoing, "slab", split_axis=0, concat_axis=0, tiled=True)
    both_sides = pl.pallas_call(
        functools.partial(chain_kernel, group_size=group_size),
        out_shape=jax.ShapeDtypeStruct(to_owner.shape, jnp.float32),
        in_specs=[pl.BlockSpec(memory_space=pltpu.SMEM)]
        + [pl.BlockSpec(memory_space=pltpu.VMEM)] * (group_size + 1),
        out_specs=pl.BlockSpec(memory_space=pltpu.VMEM),
    )(position.astype(jnp.int32).reshape(1), *across, to_owner)
    from_owner = lax.all_to_all(both_sides, "slab", split_axis=0, concat_axis=0, tiled=True)
    mine = jnp.stack([from_owner[owner] for owner in owners])
    left_values = mine[:, :, 0]
    right_values = mine[:, :, 1]

    boundary_line = jnp.concatenate([left_values, right_values], axis=2).astype(jnp.bfloat16)
    extension = jnp.einsum(
        "hg,dog->odh", extend_cols, boundary_line, preferred_element_type=jnp.float32
    )
    extension = extension.reshape(components, planes_dev, line_count - 1, point_total)
    inner_rhs = LAMBDA_TIMESTEP * velocity[:, :, 1:, :] + nonlin[:, :, 1:, :].astype(jnp.float32)
    new_inner = extension + inner_rhs / (interior_diag[None, None] + shifts[None, :, None, None])
    line_zero = jnp.swapaxes(left_values, 0, 1)
    return jnp.concatenate([line_zero[:, :, None, :], new_inner], axis=2)


def solution(mesh):
    in_specs = (
        P(None, "mode", "slab", None),
        P(None, "mode", "slab", None),
        P("slab", None),
        P("slab", None),
        P(None, "mode", "slab", None),
        P("mode", "slab", None),
        P("slab", None),
        P("slab", None),
    )
    out_specs = P(None, "mode", "slab", None)
    return jax.shard_map(
        functools.partial(on_device, slab_count=mesh.shape["slab"]), mesh=mesh, in_specs=in_specs, out_specs=out_specs, check_vma=False
    )
```

```python
import functools

import jax
import jax.numpy as jnp
from jax import lax
from jax.experimental import pallas as pl
from jax.experimental.pallas import tpu as pltpu
from jax.sharding import PartitionSpec as P

PLANES = 64


LAMBDA_TIMESTEP = 0.5
WAVE_BASE = 0.125
HIGHEST = lax.Precision.HIGHEST


def plane_numbers(planes):
    index_plane = jnp.arange(planes, dtype=jnp.int32)
    return jnp.where(index_plane == 1, planes // 2, index_plane // 2)


def plane_shift(wavenum):
    return LAMBDA_TIMESTEP + (wavenum.astype(jnp.float32) * WAVE_BASE) ** 2


def spectral_tables(planes, quad_points):
    wavenum = plane_numbers(planes)
    station = jnp.arange(quad_points, dtype=jnp.int32)
    phases = station[:, None] * wavenum[None, :] % quad_points
    angles = phases.astype(jnp.float32) * (2.0 * jnp.pi / quad_points)
    index_plane = jnp.arange(planes, dtype=jnp.int32)
    odd_plane = (index_plane % 2 == 1) & (index_plane != 1)
    inverse = jnp.where(odd_plane[None, :], -jnp.sin(angles), jnp.cos(angles))
    weights = jnp.where(index_plane == 0, 1.0, 2.0).astype(jnp.float32) / quad_points
    forward = weights[:, None] * inverse.T
    return (inverse.astype(jnp.bfloat16), forward.astype(jnp.bfloat16))


def lamb_vector(velocity_phys, vorticity_phys):
    first = velocity_phys[1] * vorticity_phys[2] - velocity_phys[2] * vorticity_phys[1]
    second = velocity_phys[2] * vorticity_phys[0] - velocity_phys[0] * vorticity_phys[2]
    third = velocity_phys[0] * vorticity_phys[1] - velocity_phys[1] * vorticity_phys[0]
    return jnp.stack([first, second, third])


def chain_kernel(position_ref, *refs, group_size):
    group_refs = refs[:group_size]
    sides_ref, out_ref = refs[group_size:]
    slab_count = sides_ref.shape[0]

    def apply(matrix, vectors):
        return lax.dot_general(
            vectors,
            matrix,
            (((1,), (1,)), ((), ())),
            precision=lax.Precision.HIGH,
            preferred_element_type=jnp.float32,
        )

    def solve(position):
        def blocks_of(slab):
            label = (slab + 1) % slab_count
            group_slot = (label % group_size - 1) % group_size
            spot_slot = (label // group_size - position) % group_size
            return group_refs[group_slot].at[spot_slot]

        zero = jnp.zeros(sides_ref.shape[2:], jnp.float32)
        forward_values = [zero]
        for k in range(1, slab_count):
            source = sides_ref[k, 0] + sides_ref[k - 1, 1]
            forward_values.append(source - apply(blocks_of(k)[0], forward_values[-1]))
        after = zero
        for k in range(slab_count - 1, 0, -1):
            blocks = blocks_of(k)
            solved = apply(blocks[2], forward_values[k]) - apply(blocks[1], after)
            out_ref[k, 0] = solved
            out_ref[k, 1] = after
            after = solved
        out_ref[0, 0] = zero
        out_ref[0, 1] = after

    for position in range(group_size):
        pl.when(position_ref[0] == position)(functools.partial(solve, position))


def on_device(
    velocity,
    vorticity,
    lift,
    extend,
    interface_chain_factors,
    pivot_inverse,
    interior_diag,
    node_map,
    *,
    slab_count,
):
    components, planes_dev, line_count, point_total = velocity.shape
    quad_points = 3 * PLANES // 2
    slab_index = lax.axis_index("slab")
    group_size = planes_dev
    group_count = slab_count // group_size
    position = ((slab_index + 1) % slab_count) // group_size

    def slab_of(label):
        return (label - 1) % slab_count

    owners = [slab_of(plane * group_size + 1) for plane in range(planes_dev)]

    blocks = jnp.stack(
        [interface_chain_factors[0], interface_chain_factors[1], pivot_inverse], axis=1
    )
    within = [blocks[position]]
    for offset in range(1, group_count):
        pairs = [
            (
                slab_of(rest + group_size * rank),
                slab_of(rest + group_size * ((rank - offset) % group_count)),
            )
            for rest in range(group_size)
            for rank in range(group_count)
        ]
        within.append(lax.ppermute(blocks[(position - offset) % group_count], "slab", pairs))
    group_blocks = jnp.stack(within)

    halfway_offsets = jnp.concatenate(
        [jnp.zeros((point_total,), jnp.int32), jnp.full((point_total,), point_total, jnp.int32)]
    )
    row_order = node_map[0] + halfway_offsets
    one_hot = (
        row_order[:, None] == jnp.arange(2 * point_total, dtype=jnp.int32)[None, :]
    ).astype(jnp.bfloat16)
    lift_rows = jnp.einsum(
        "ir,rf->if", one_hot, lift, preferred_element_type=jnp.float32
    ).astype(jnp.bfloat16)
    extend_cols = jnp.einsum(
        "hr,ir->hi", extend, one_hot, preferred_element_type=jnp.float32
    ).astype(jnp.bfloat16)

    inverse, forward = spectral_tables(PLANES, quad_points)
    wavenum = lax.dynamic_slice_in_dim(
        plane_numbers(PLANES), lax.axis_index("mode") * planes_dev, planes_dev
    )
    shifts = plane_shift(wavenum)
    velocity_half = velocity.astype(jnp.bfloat16)
    both_fields = jnp.concatenate([velocity_half, vorticity], axis=0)
    field_lines = lax.all_to_all(both_fields, "mode", split_axis=2, concat_axis=1, tiled=True)
    group_blocks, field_lines = lax.optimization_barrier((group_blocks, field_lines))
    across = [group_blocks]
    for offset in range(1, group_size):
        pairs = [
            (slab_of(plane * group_size + (1 + offset) % group_size), owners[plane])
            for plane in range(planes_dev)
        ]
        across.append(lax.ppermute(group_blocks, "slab", pairs))
    phys = jnp.einsum("qp,cplb->cqlb", inverse, field_lines, preferred_element_type=jnp.float32)
    lamb_field = lamb_vector(phys[:components], phys[components:]).astype(jnp.bfloat16)
    nonlin_lines = jnp.einsum(
        "pq,cqlb->cplb", forward, lamb_field, preferred_element_type=jnp.float32
    ).astype(jnp.bfloat16)
    interior_point_velocity = (
        (LAMBDA_TIMESTEP * velocity[:, :, 1:, :])
        .astype(jnp.bfloat16)
        .reshape(components, planes_dev, -1)
    )
    lifted_velocity = jnp.einsum(
        "hf,vqf->qvh", lift_rows, interior_point_velocity, preferred_element_type=jnp.float32
    )
    nonlin = lax.all_to_all(nonlin_lines, "mode", split_axis=1, concat_axis=2, tiled=True)
    inner_nonlinear_term = nonlin[:, :, 1:, :].reshape(components, planes_dev, -1)
    cond_line = lifted_velocity + jnp.einsum(
        "hf,vqf->qvh", lift_rows, inner_nonlinear_term, preferred_element_type=jnp.float32
    )
    line_zero_rhs = jnp.swapaxes(
        LAMBDA_TIMESTEP * velocity[:, :, 0, :] + nonlin[:, :, 0, :].astype(jnp.float32), 0, 1
    )
    rhs_left = cond_line[:, :, :point_total] + line_zero_rhs
    right_part = cond_line[:, :, point_total:]

    sides = jnp.stack([rhs_left, right_part], axis=1)
    across, sides = lax.optimization_barrier((across, sides))
    destination_plane = [owners.index(slab) if slab in owners else 0 for slab in range(slab_count)]
    outgoing = jnp.stack([sides[plane] for plane in destination_plane])
    to_owner = lax.all_to_all(outgoing, "slab", split_axis=0, concat_axis=0, tiled=True)
    both_sides = pl.pallas_call(
        functools.partial(chain_kernel, group_size=group_size),
        out_shape=jax.ShapeDtypeStruct(to_owner.shape, jnp.float32),
        in_specs=[pl.BlockSpec(memory_space=pltpu.SMEM)]
        + [pl.BlockSpec(memory_space=pltpu.VMEM)] * (group_size + 1),
        out_specs=pl.BlockSpec(memory_space=pltpu.VMEM),
    )(position.astype(jnp.int32).reshape(1), *across, to_owner)
    from_owner = lax.all_to_all(both_sides, "slab", split_axis=0, concat_axis=0, tiled=True)
    mine = jnp.stack([from_owner[owner] for owner in owners])
    left_values = mine[:, 0]
    right_values = mine[:, 1]

    boundary_line = jnp.concatenate([left_values, right_values], axis=2).astype(jnp.bfloat16)
    extension = jnp.einsum(
        "hg,dog->odh", extend_cols, boundary_line, preferred_element_type=jnp.float32
    )
    extension = extension.reshape(components, planes_dev, line_count - 1, point_total)
    inner_rhs = LAMBDA_TIMESTEP * velocity[:, :, 1:, :] + nonlin[:, :, 1:, :].astype(jnp.float32)
    new_inner = extension + inner_rhs / (interior_diag[None, None] + shifts[None, :, None, None])
    line_zero = jnp.swapaxes(left_values, 0, 1)
    return jnp.concatenate([line_zero[:, :, None, :], new_inner], axis=2)


def solution(mesh):
    in_specs = (
        P(None, "mode", "slab", None),
        P(None, "mode", "slab", None),
        P("slab", None),
        P("slab", None),
        P(None, "mode", "slab", None),
        P("mode", "slab", None),
        P("slab", None),
        P("slab", None),
    )
    out_specs = P(None, "mode", "slab", None)
    return jax.shard_map(
        functools.partial(on_device, slab_count=mesh.shape["slab"]), mesh=mesh, in_specs=in_specs, out_specs=out_specs, check_vma=False
    )
```

```python
import functools

import jax
import jax.numpy as jnp
from jax import lax
from jax.experimental import pallas as pl
from jax.experimental.pallas import tpu as pltpu
from jax.sharding import PartitionSpec as P

PLANES = 64


LAMBDA_TIMESTEP = 0.5
WAVE_BASE = 0.125
HIGHEST = lax.Precision.HIGHEST


def plane_numbers(planes):
    index_plane = jnp.arange(planes, dtype=jnp.int32)
    return jnp.where(index_plane == 1, planes // 2, index_plane // 2)


def plane_shift(wavenum):
    return LAMBDA_TIMESTEP + (wavenum.astype(jnp.float32) * WAVE_BASE) ** 2


def spectral_tables(planes, quad_points):
    wavenum = plane_numbers(planes)
    station = jnp.arange(quad_points, dtype=jnp.int32)
    phases = station[:, None] * wavenum[None, :] % quad_points
    angles = phases.astype(jnp.float32) * (2.0 * jnp.pi / quad_points)
    index_plane = jnp.arange(planes, dtype=jnp.int32)
    odd_plane = (index_plane % 2 == 1) & (index_plane != 1)
    inverse = jnp.where(odd_plane[None, :], -jnp.sin(angles), jnp.cos(angles))
    weights = jnp.where(index_plane == 0, 1.0, 2.0).astype(jnp.float32) / quad_points
    forward = weights[:, None] * inverse.T
    return (inverse.astype(jnp.bfloat16), forward.astype(jnp.bfloat16))


def lamb_vector(velocity_phys, vorticity_phys):
    first = velocity_phys[1] * vorticity_phys[2] - velocity_phys[2] * vorticity_phys[1]
    second = velocity_phys[2] * vorticity_phys[0] - velocity_phys[0] * vorticity_phys[2]
    third = velocity_phys[0] * vorticity_phys[1] - velocity_phys[1] * vorticity_phys[0]
    return jnp.stack([first, second, third])


def chain_kernel(position_ref, *refs, group_size):
    group_refs = refs[:group_size]
    sides_ref, out_ref = refs[group_size:]
    slab_count = sides_ref.shape[0]

    def apply(matrix, vectors):
        return lax.dot_general(
            vectors,
            matrix,
            (((1,), (1,)), ((), ())),
            precision=lax.Precision.HIGH,
            preferred_element_type=jnp.float32,
        )

    def solve(position):
        def blocks_of(slab):
            label = (slab + 1) % slab_count
            group_slot = (label % group_size - 1) % group_size
            spot_slot = (label // group_size - position) % group_size
            return group_refs[group_slot].at[spot_slot]

        zero = jnp.zeros(sides_ref.shape[2:], jnp.float32)
        forward_values = [zero]
        for k in range(1, slab_count):
            source = sides_ref[k, 0] + sides_ref[k - 1, 1]
            forward_values.append(source - apply(blocks_of(k)[0], forward_values[-1]))
        after = zero
        for k in range(slab_count - 1, 0, -1):
            blocks = blocks_of(k)
            solved = apply(blocks[2], forward_values[k]) - apply(blocks[1], after)
            out_ref[k] = jnp.stack([solved, after], axis=1)
            after = solved
        out_ref[0] = jnp.stack([zero, after], axis=1)

    for position in range(group_size):
        pl.when(position_ref[0] == position)(functools.partial(solve, position))


def on_device(
    velocity,
    vorticity,
    lift,
    extend,
    interface_chain_factors,
    pivot_inverse,
    interior_diag,
    node_map,
    *,
    slab_count,
):
    components, planes_dev, line_count, point_total = velocity.shape
    quad_points = 3 * PLANES // 2
    slab_index = lax.axis_index("slab")
    group_size = planes_dev
    group_count = slab_count // group_size
    position = ((slab_index + 1) % slab_count) // group_size

    def slab_of(label):
        return (label - 1) % slab_count

    owners = [slab_of(plane * group_size + 1) for plane in range(planes_dev)]

    blocks = jnp.stack(
        [interface_chain_factors[0], interface_chain_factors[1], pivot_inverse], axis=1
    )
    within = [blocks[position]]
    for offset in range(1, group_count):
        pairs = [
            (
                slab_of(rest + group_size * rank),
                slab_of(rest + group_size * ((rank - offset) % group_count)),
            )
            for rest in range(group_size)
            for rank in range(group_count)
        ]
        within.append(lax.ppermute(blocks[(position - offset) % group_count], "slab", pairs))
    group_blocks = jnp.stack(within)

    halfway_offsets = jnp.concatenate(
        [jnp.zeros((point_total,), jnp.int32), jnp.full((point_total,), point_total, jnp.int32)]
    )
    row_order = node_map[0] + halfway_offsets
    one_hot = (
        row_order[:, None] == jnp.arange(2 * point_total, dtype=jnp.int32)[None, :]
    ).astype(jnp.bfloat16)
    lift_rows = jnp.einsum(
        "ir,rf->if", one_hot, lift, preferred_element_type=jnp.float32
    ).astype(jnp.bfloat16)
    extend_cols = jnp.einsum(
        "hr,ir->hi", extend, one_hot, preferred_element_type=jnp.float32
    ).astype(jnp.bfloat16)

    inverse, forward = spectral_tables(PLANES, quad_points)
    wavenum = lax.dynamic_slice_in_dim(
        plane_numbers(PLANES), lax.axis_index("mode") * planes_dev, planes_dev
    )
    shifts = plane_shift(wavenum)
    velocity_half = velocity.astype(jnp.bfloat16)
    both_fields = jnp.concatenate([velocity_half, vorticity], axis=0)
    field_lines = lax.all_to_all(both_fields, "mode", split_axis=2, concat_axis=1, tiled=True)
    group_blocks, field_lines = lax.optimization_barrier((group_blocks, field_lines))
    across = [group_blocks]
    for offset in range(1, group_size):
        pairs = [
            (slab_of(plane * group_size + (1 + offset) % group_size), owners[plane])
            for plane in range(planes_dev)
        ]
        across.append(lax.ppermute(group_blocks, "slab", pairs))
    phys = jnp.einsum("qp,cplb->cqlb", inverse, field_lines, preferred_element_type=jnp.float32)
    lamb_field = lamb_vector(phys[:components], phys[components:]).astype(jnp.bfloat16)
    nonlin_lines = jnp.einsum(
        "pq,cqlb->cplb", forward, lamb_field, preferred_element_type=jnp.float32
    ).astype(jnp.bfloat16)
    interior_point_velocity = (
        (LAMBDA_TIMESTEP * velocity[:, :, 1:, :])
        .astype(jnp.bfloat16)
        .reshape(components, planes_dev, -1)
    )
    lifted_velocity = jnp.einsum(
        "hf,vqf->qvh", lift_rows, interior_point_velocity, preferred_element_type=jnp.float32
    )
    nonlin = lax.all_to_all(nonlin_lines, "mode", split_axis=1, concat_axis=2, tiled=True)
    inner_nonlinear_term = nonlin[:, :, 1:, :].reshape(components, planes_dev, -1)
    cond_line = lifted_velocity + jnp.einsum(
        "hf,vqf->qvh", lift_rows, inner_nonlinear_term, preferred_element_type=jnp.float32
    )
    line_zero_rhs = jnp.swapaxes(
        LAMBDA_TIMESTEP * velocity[:, :, 0, :] + nonlin[:, :, 0, :].astype(jnp.float32), 0, 1
    )
    rhs_left = cond_line[:, :, :point_total] + line_zero_rhs
    right_part = cond_line[:, :, point_total:]

    sides = jnp.stack([rhs_left, right_part], axis=1)
    destination_plane = [owners.index(slab) if slab in owners else 0 for slab in range(slab_count)]
    outgoing = jnp.stack([sides[plane] for plane in destination_plane])
    to_owner = lax.all_to_all(outgoing, "slab", split_axis=0, concat_axis=0, tiled=True)
    both_sides = pl.pallas_call(
        functools.partial(chain_kernel, group_size=group_size),
        out_shape=jax.ShapeDtypeStruct(
            (slab_count, components, 2, point_total), jnp.float32
        ),
        in_specs=[pl.BlockSpec(memory_space=pltpu.SMEM)]
        + [pl.BlockSpec(memory_space=pltpu.VMEM)] * (group_size + 1),
        out_specs=pl.BlockSpec(memory_space=pltpu.VMEM),
    )(position.astype(jnp.int32).reshape(1), *across, to_owner)
    from_owner = lax.all_to_all(both_sides, "slab", split_axis=0, concat_axis=0, tiled=True)
    mine = jnp.stack([from_owner[owner] for owner in owners])
    left_values = mine[:, :, 0]
    right_values = mine[:, :, 1]

    boundary_line = jnp.concatenate([left_values, right_values], axis=2).astype(jnp.bfloat16)
    extension = jnp.einsum(
        "hg,dog->odh", extend_cols, boundary_line, preferred_element_type=jnp.float32
    )
    extension = extension.reshape(components, planes_dev, line_count - 1, point_total)
    inner_rhs = LAMBDA_TIMESTEP * velocity[:, :, 1:, :] + nonlin[:, :, 1:, :].astype(jnp.float32)
    new_inner = extension + inner_rhs / (interior_diag[None, None] + shifts[None, :, None, None])
    line_zero = jnp.swapaxes(left_values, 0, 1)
    return jnp.concatenate([line_zero[:, :, None, :], new_inner], axis=2)


def solution(mesh):
    in_specs = (
        P(None, "mode", "slab", None),
        P(None, "mode", "slab", None),
        P("slab", None),
        P("slab", None),
        P(None, "mode", "slab", None),
        P("mode", "slab", None),
        P("slab", None),
        P("slab", None),
    )
    out_specs = P(None, "mode", "slab", None)
    return jax.shard_map(
        functools.partial(on_device, slab_count=mesh.shape["slab"]), mesh=mesh, in_specs=in_specs, out_specs=out_specs, check_vma=False
    )
```

```python
import functools

import jax
import jax.numpy as jnp
from jax import lax
from jax.experimental import pallas as pl
from jax.experimental.pallas import tpu as pltpu
from jax.sharding import PartitionSpec as P

PLANES = 64


LAMBDA_TIMESTEP = 0.5
WAVE_BASE = 0.125
HIGHEST = lax.Precision.HIGHEST


def plane_numbers(planes):
    index_plane = jnp.arange(planes, dtype=jnp.int32)
    return jnp.where(index_plane == 1, planes // 2, index_plane // 2)


def plane_shift(wavenum):
    return LAMBDA_TIMESTEP + (wavenum.astype(jnp.float32) * WAVE_BASE) ** 2


def spectral_tables(planes, quad_points):
    wavenum = plane_numbers(planes)
    station = jnp.arange(quad_points, dtype=jnp.int32)
    phases = station[:, None] * wavenum[None, :] % quad_points
    angles = phases.astype(jnp.float32) * (2.0 * jnp.pi / quad_points)
    index_plane = jnp.arange(planes, dtype=jnp.int32)
    odd_plane = (index_plane % 2 == 1) & (index_plane != 1)
    inverse = jnp.where(odd_plane[None, :], -jnp.sin(angles), jnp.cos(angles))
    weights = jnp.where(index_plane == 0, 1.0, 2.0).astype(jnp.float32) / quad_points
    forward = weights[:, None] * inverse.T
    return (inverse.astype(jnp.bfloat16), forward.astype(jnp.bfloat16))


def lamb_vector(velocity_phys, vorticity_phys):
    first = velocity_phys[1] * vorticity_phys[2] - velocity_phys[2] * vorticity_phys[1]
    second = velocity_phys[2] * vorticity_phys[0] - velocity_phys[0] * vorticity_phys[2]
    third = velocity_phys[0] * vorticity_phys[1] - velocity_phys[1] * vorticity_phys[0]
    return jnp.stack([first, second, third])


def chain_kernel(position_ref, *refs, group_size):
    group_refs = refs[:group_size]
    sides_ref, out_ref = refs[group_size:]
    slab_count = sides_ref.shape[0]

    def apply(matrix, vectors):
        return lax.dot_general(
            vectors,
            matrix,
            (((1,), (1,)), ((), ())),
            precision=lax.Precision.HIGH,
            preferred_element_type=jnp.float32,
        )

    def solve(position):
        def blocks_of(slab):
            label = (slab + 1) % slab_count
            group_slot = (label % group_size - 1) % group_size
            spot_slot = (label // group_size - position) % group_size
            return group_refs[group_slot].at[spot_slot]

        zero = jnp.zeros(sides_ref.shape[2:], jnp.float32)
        forward_values = [zero]
        for k in range(1, slab_count):
            source = sides_ref[k, 0] + sides_ref[k - 1, 1]
            forward_values.append(source - apply(blocks_of(k)[0], forward_values[-1]))
        after = zero
        for k in range(slab_count - 1, 0, -1):
            blocks = blocks_of(k)
            solved = apply(blocks[2], forward_values[k]) - apply(blocks[1], after)
            out_ref[k] = jnp.stack([solved, after], axis=1)
            after = solved
        out_ref[0] = jnp.stack([zero, after], axis=1)

    for position in range(group_size):
        pl.when(position_ref[0] == position)(functools.partial(solve, position))


def on_device(
    velocity,
    vorticity,
    lift,
    extend,
    interface_chain_factors,
    pivot_inverse,
    interior_diag,
    node_map,
    *,
    slab_count,
):
    components, planes_dev, line_count, point_total = velocity.shape
    quad_points = 3 * PLANES // 2
    slab_index = lax.axis_index("slab")
    group_size = planes_dev
    group_count = slab_count // group_size
    position = ((slab_index + 1) % slab_count) // group_size

    def slab_of(label):
        return (label - 1) % slab_count

    owners = [slab_of(plane * group_size + 1) for plane in range(planes_dev)]

    blocks = jnp.stack(
        [interface_chain_factors[0], interface_chain_factors[1], pivot_inverse], axis=1
    )
    within = [blocks[position]]
    for offset in range(1, group_count):
        pairs = [
            (
                slab_of(rest + group_size * rank),
                slab_of(rest + group_size * ((rank - offset) % group_count)),
            )
            for rest in range(group_size)
            for rank in range(group_count)
        ]
        within.append(lax.ppermute(blocks[(position - offset) % group_count], "slab", pairs))

    halfway_offsets = jnp.concatenate(
        [jnp.zeros((point_total,), jnp.int32), jnp.full((point_total,), point_total, jnp.int32)]
    )
    row_order = node_map[0] + halfway_offsets
    one_hot = (
        row_order[:, None] == jnp.arange(2 * point_total, dtype=jnp.int32)[None, :]
    ).astype(jnp.bfloat16)
    lift_rows = jnp.einsum(
        "ir,rf->if", one_hot, lift, preferred_element_type=jnp.float32
    ).astype(jnp.bfloat16)
    extend_cols = jnp.einsum(
        "hr,ir->hi", extend, one_hot, preferred_element_type=jnp.float32
    ).astype(jnp.bfloat16)

    inverse, forward = spectral_tables(PLANES, quad_points)
    wavenum = lax.dynamic_slice_in_dim(
        plane_numbers(PLANES), lax.axis_index("mode") * planes_dev, planes_dev
    )
    shifts = plane_shift(wavenum)
    velocity_half = velocity.astype(jnp.bfloat16)
    both_fields = jnp.concatenate([velocity_half, vorticity], axis=0)
    field_lines = lax.all_to_all(both_fields, "mode", split_axis=2, concat_axis=1, tiled=True)
    within, field_lines = lax.optimization_barrier((tuple(within), field_lines))
    group_blocks = jnp.stack(within)
    across = [group_blocks]
    for offset in range(1, group_size):
        pairs = [
            (slab_of(plane * group_size + (1 + offset) % group_size), owners[plane])
            for plane in range(planes_dev)
        ]
        across.append(lax.ppermute(group_blocks, "slab", pairs))
    phys = jnp.einsum("qp,cplb->cqlb", inverse, field_lines, preferred_element_type=jnp.float32)
    lamb_field = lamb_vector(phys[:components], phys[components:]).astype(jnp.bfloat16)
    nonlin_lines = jnp.einsum(
        "pq,cqlb->cplb", forward, lamb_field, preferred_element_type=jnp.float32
    ).astype(jnp.bfloat16)
    interior_point_velocity = (
        (LAMBDA_TIMESTEP * velocity[:, :, 1:, :])
        .astype(jnp.bfloat16)
        .reshape(components, planes_dev, -1)
    )
    lifted_velocity = jnp.einsum(
        "hf,vqf->qvh", lift_rows, interior_point_velocity, preferred_element_type=jnp.float32
    )
    nonlin = lax.all_to_all(nonlin_lines, "mode", split_axis=1, concat_axis=2, tiled=True)
    inner_nonlinear_term = nonlin[:, :, 1:, :].reshape(components, planes_dev, -1)
    cond_line = lifted_velocity + jnp.einsum(
        "hf,vqf->qvh", lift_rows, inner_nonlinear_term, preferred_element_type=jnp.float32
    )
    line_zero_rhs = jnp.swapaxes(
        LAMBDA_TIMESTEP * velocity[:, :, 0, :] + nonlin[:, :, 0, :].astype(jnp.float32), 0, 1
    )
    rhs_left = cond_line[:, :, :point_total] + line_zero_rhs
    right_part = cond_line[:, :, point_total:]

    sides = jnp.stack([rhs_left, right_part], axis=1)
    destination_plane = [owners.index(slab) if slab in owners else 0 for slab in range(slab_count)]
    outgoing = jnp.stack([sides[plane] for plane in destination_plane])
    to_owner = lax.all_to_all(outgoing, "slab", split_axis=0, concat_axis=0, tiled=True)
    both_sides = pl.pallas_call(
        functools.partial(chain_kernel, group_size=group_size),
        out_shape=jax.ShapeDtypeStruct(
            (slab_count, components, 2, point_total), jnp.float32
        ),
        in_specs=[pl.BlockSpec(memory_space=pltpu.SMEM)]
        + [pl.BlockSpec(memory_space=pltpu.VMEM)] * (group_size + 1),
        out_specs=pl.BlockSpec(memory_space=pltpu.VMEM),
    )(position.astype(jnp.int32).reshape(1), *across, to_owner)
    from_owner = lax.all_to_all(both_sides, "slab", split_axis=0, concat_axis=0, tiled=True)
    mine = jnp.stack([from_owner[owner] for owner in owners])
    left_values = mine[:, :, 0]
    right_values = mine[:, :, 1]

    boundary_line = jnp.concatenate([left_values, right_values], axis=2).astype(jnp.bfloat16)
    extension = jnp.einsum(
        "hg,dog->odh", extend_cols, boundary_line, preferred_element_type=jnp.float32
    )
    extension = extension.reshape(components, planes_dev, line_count - 1, point_total)
    inner_rhs = LAMBDA_TIMESTEP * velocity[:, :, 1:, :] + nonlin[:, :, 1:, :].astype(jnp.float32)
    new_inner = extension + inner_rhs / (interior_diag[None, None] + shifts[None, :, None, None])
    line_zero = jnp.swapaxes(left_values, 0, 1)
    return jnp.concatenate([line_zero[:, :, None, :], new_inner], axis=2)


def solution(mesh):
    in_specs = (
        P(None, "mode", "slab", None),
        P(None, "mode", "slab", None),
        P("slab", None),
        P("slab", None),
        P(None, "mode", "slab", None),
        P("mode", "slab", None),
        P("slab", None),
        P("slab", None),
    )
    out_specs = P(None, "mode", "slab", None)
    return jax.shard_map(
        functools.partial(on_device, slab_count=mesh.shape["slab"]), mesh=mesh, in_specs=in_specs, out_specs=out_specs, check_vma=False
    )
```

```python
import functools

import jax
import jax.numpy as jnp
from jax import lax
from jax.experimental import pallas as pl
from jax.experimental.pallas import tpu as pltpu
from jax.sharding import PartitionSpec as P

PLANES = 64


LAMBDA_TIMESTEP = 0.5
WAVE_BASE = 0.125
HIGHEST = lax.Precision.HIGHEST


def plane_numbers(planes):
    index_plane = jnp.arange(planes, dtype=jnp.int32)
    return jnp.where(index_plane == 1, planes // 2, index_plane // 2)


def plane_shift(wavenum):
    return LAMBDA_TIMESTEP + (wavenum.astype(jnp.float32) * WAVE_BASE) ** 2


def spectral_tables(planes, quad_points):
    wavenum = plane_numbers(planes)
    station = jnp.arange(quad_points, dtype=jnp.int32)
    phases = station[:, None] * wavenum[None, :] % quad_points
    angles = phases.astype(jnp.float32) * (2.0 * jnp.pi / quad_points)
    index_plane = jnp.arange(planes, dtype=jnp.int32)
    odd_plane = (index_plane % 2 == 1) & (index_plane != 1)
    inverse = jnp.where(odd_plane[None, :], -jnp.sin(angles), jnp.cos(angles))
    weights = jnp.where(index_plane == 0, 1.0, 2.0).astype(jnp.float32) / quad_points
    forward = weights[:, None] * inverse.T
    return (inverse.astype(jnp.bfloat16), forward.astype(jnp.bfloat16))


def lamb_vector(velocity_phys, vorticity_phys):
    first = velocity_phys[1] * vorticity_phys[2] - velocity_phys[2] * vorticity_phys[1]
    second = velocity_phys[2] * vorticity_phys[0] - velocity_phys[0] * vorticity_phys[2]
    third = velocity_phys[0] * vorticity_phys[1] - velocity_phys[1] * vorticity_phys[0]
    return jnp.stack([first, second, third])


def chain_kernel(position_ref, *refs, group_size):
    group_refs = refs[:group_size]
    sides_ref, out_ref = refs[group_size:]
    slab_count = sides_ref.shape[0]

    def apply(matrix, vectors):
        return lax.dot_general(
            vectors,
            matrix,
            (((1,), (1,)), ((), ())),
            precision=lax.Precision.HIGH,
            preferred_element_type=jnp.float32,
        )

    def solve(position):
        def blocks_of(slab):
            label = (slab + 1) % slab_count
            group_slot = (label % group_size - 1) % group_size
            spot_slot = (label // group_size - position) % group_size
            return group_refs[group_slot].at[spot_slot]

        zero = jnp.zeros(sides_ref.shape[2:], jnp.float32)
        forward_values = [zero]
        for k in range(1, slab_count):
            source = sides_ref[k, 0] + sides_ref[k - 1, 1]
            forward_values.append(source - apply(blocks_of(k)[0], forward_values[-1]))
        after = zero
        for k in range(slab_count - 1, 0, -1):
            blocks = blocks_of(k)
            solved = apply(blocks[2], forward_values[k]) - apply(blocks[1], after)
            out_ref[k] = jnp.stack([solved, after], axis=1)
            after = solved
        out_ref[0] = jnp.stack([zero, after], axis=1)

    for position in range(group_size):
        pl.when(position_ref[0] == position)(functools.partial(solve, position))


def on_device(
    velocity,
    vorticity,
    lift,
    extend,
    interface_chain_factors,
    pivot_inverse,
    interior_diag,
    node_map,
    *,
    slab_count,
):
    components, planes_dev, line_count, point_total = velocity.shape
    quad_points = 3 * PLANES // 2
    slab_index = lax.axis_index("slab")
    group_size = planes_dev
    group_count = slab_count // group_size
    position = ((slab_index + 1) % slab_count) // group_size

    def slab_of(label):
        return (label - 1) % slab_count

    owners = [slab_of(plane * group_size + 1) for plane in range(planes_dev)]

    blocks = jnp.stack(
        [interface_chain_factors[0], interface_chain_factors[1], pivot_inverse], axis=1
    )
    within = [blocks[position]]
    for offset in range(1, group_count):
        pairs = [
            (
                slab_of(rest + group_size * rank),
                slab_of(rest + group_size * ((rank - offset) % group_count)),
            )
            for rest in range(group_size)
            for rank in range(group_count)
        ]
        within.append(lax.ppermute(blocks[(position - offset) % group_count], "slab", pairs))

    halfway_offsets = jnp.concatenate(
        [jnp.zeros((point_total,), jnp.int32), jnp.full((point_total,), point_total, jnp.int32)]
    )
    row_order = node_map[0] + halfway_offsets
    one_hot = (
        row_order[:, None] == jnp.arange(2 * point_total, dtype=jnp.int32)[None, :]
    ).astype(jnp.bfloat16)
    lift_rows = jnp.einsum(
        "ir,rf->if", one_hot, lift, preferred_element_type=jnp.float32
    ).astype(jnp.bfloat16)
    extend_cols = jnp.einsum(
        "hr,ir->hi", extend, one_hot, preferred_element_type=jnp.float32
    ).astype(jnp.bfloat16)

    inverse, forward = spectral_tables(PLANES, quad_points)
    wavenum = lax.dynamic_slice_in_dim(
        plane_numbers(PLANES), lax.axis_index("mode") * planes_dev, planes_dev
    )
    shifts = plane_shift(wavenum)
    velocity_half = velocity.astype(jnp.bfloat16)
    both_fields = jnp.concatenate([velocity_half, vorticity], axis=0)
    field_lines = lax.all_to_all(both_fields, "mode", split_axis=2, concat_axis=1, tiled=True)
    within, field_lines = lax.optimization_barrier((tuple(within), field_lines))
    group_blocks = jnp.stack(within)
    across = [group_blocks]
    for offset in range(1, group_size):
        pairs = [
            (slab_of(plane * group_size + (1 + offset) % group_size), owners[plane])
            for plane in range(planes_dev)
        ]
        across.append(lax.ppermute(group_blocks, "slab", pairs))
    phys = jnp.einsum("qp,cplb->cqlb", inverse, field_lines, preferred_element_type=jnp.float32)
    lamb_field = lamb_vector(phys[:components], phys[components:]).astype(jnp.bfloat16)
    nonlin_lines = jnp.einsum(
        "pq,cqlb->cplb", forward, lamb_field, preferred_element_type=jnp.float32
    ).astype(jnp.bfloat16)
    interior_point_velocity = (
        (LAMBDA_TIMESTEP * velocity[:, :, 1:, :])
        .astype(jnp.bfloat16)
        .reshape(components, planes_dev, -1)
    )
    lifted_velocity = jnp.einsum(
        "hf,vqf->qvh", lift_rows, interior_point_velocity, preferred_element_type=jnp.float32
    )
    nonlin = lax.all_to_all(nonlin_lines, "mode", split_axis=1, concat_axis=2, tiled=True)
    inner_nonlinear_term = nonlin[:, :, 1:, :].reshape(components, planes_dev, -1)
    cond_line = lifted_velocity + jnp.einsum(
        "hf,vqf->qvh", lift_rows, inner_nonlinear_term, preferred_element_type=jnp.float32
    )
    line_zero_rhs = jnp.swapaxes(
        LAMBDA_TIMESTEP * velocity[:, :, 0, :] + nonlin[:, :, 0, :].astype(jnp.float32), 0, 1
    )
    rhs_left = cond_line[:, :, :point_total] + line_zero_rhs
    right_part = cond_line[:, :, point_total:]

    sides = jnp.stack([rhs_left, right_part], axis=1)
    destination_plane = [owners.index(slab) if slab in owners else 0 for slab in range(slab_count)]
    outgoing = jnp.stack([sides[plane] for plane in destination_plane])
    to_owner = lax.all_to_all(outgoing, "slab", split_axis=0, concat_axis=0, tiled=True)
    both_sides = pl.pallas_call(
        functools.partial(chain_kernel, group_size=group_size),
        out_shape=jax.ShapeDtypeStruct(
            (slab_count, components, 2, point_total), jnp.float32
        ),
        in_specs=[pl.BlockSpec(memory_space=pltpu.SMEM)]
        + [pl.BlockSpec(memory_space=pltpu.VMEM)] * (group_size + 1),
        out_specs=pl.BlockSpec(memory_space=pltpu.VMEM),
    )(position.astype(jnp.int32).reshape(1), *across, to_owner)
    from_owner = lax.all_to_all(both_sides, "slab", split_axis=0, concat_axis=0, tiled=True)
    mine = jnp.stack([from_owner[owner] for owner in owners])
    left_values = mine[:, :, 0]
    right_values = mine[:, :, 1]

    boundary_line = jnp.concatenate([left_values, right_values], axis=2).astype(jnp.bfloat16)
    extend_lines = jnp.pad(extend_cols, ((point_total, 0), (0, 0)))
    extension = jnp.einsum(
        "hg,dog->odh", extend_lines, boundary_line, preferred_element_type=jnp.float32
    )
    extension = extension.reshape(components, planes_dev, line_count, point_total)
    inner_rhs = LAMBDA_TIMESTEP * velocity[:, :, 1:, :] + nonlin[:, :, 1:, :].astype(jnp.float32)
    scaled = inner_rhs / (interior_diag[None, None] + shifts[None, :, None, None])
    interior = jnp.pad(scaled, ((0, 0), (0, 0), (1, 0), (0, 0)))
    line_zero = jnp.swapaxes(left_values, 0, 1)
    walls = jnp.pad(line_zero[:, :, None, :], ((0, 0), (0, 0), (0, line_count - 1), (0, 0)))
    return extension + interior + walls


def solution(mesh):
    in_specs = (
        P(None, "mode", "slab", None),
        P(None, "mode", "slab", None),
        P("slab", None),
        P("slab", None),
        P(None, "mode", "slab", None),
        P("mode", "slab", None),
        P("slab", None),
        P("slab", None),
    )
    out_specs = P(None, "mode", "slab", None)
    return jax.shard_map(
        functools.partial(on_device, slab_count=mesh.shape["slab"]), mesh=mesh, in_specs=in_specs, out_specs=out_specs, check_vma=False
    )
```

```python
import functools

import jax
import jax.numpy as jnp
from jax import lax
from jax.experimental import pallas as pl
from jax.experimental.pallas import tpu as pltpu
from jax.sharding import PartitionSpec as P

PLANES = 64


LAMBDA_TIMESTEP = 0.5
WAVE_BASE = 0.125
HIGHEST = lax.Precision.HIGHEST


def plane_numbers(planes):
    index_plane = jnp.arange(planes, dtype=jnp.int32)
    return jnp.where(index_plane == 1, planes // 2, index_plane // 2)


def plane_shift(wavenum):
    return LAMBDA_TIMESTEP + (wavenum.astype(jnp.float32) * WAVE_BASE) ** 2


def spectral_tables(planes, quad_points):
    wavenum = plane_numbers(planes)
    station = jnp.arange(quad_points, dtype=jnp.int32)
    phases = station[:, None] * wavenum[None, :] % quad_points
    angles = phases.astype(jnp.float32) * (2.0 * jnp.pi / quad_points)
    index_plane = jnp.arange(planes, dtype=jnp.int32)
    odd_plane = (index_plane % 2 == 1) & (index_plane != 1)
    inverse = jnp.where(odd_plane[None, :], -jnp.sin(angles), jnp.cos(angles))
    weights = jnp.where(index_plane == 0, 1.0, 2.0).astype(jnp.float32) / quad_points
    forward = weights[:, None] * inverse.T
    return (inverse.astype(jnp.bfloat16), forward.astype(jnp.bfloat16))


def lamb_vector(velocity_phys, vorticity_phys):
    first = velocity_phys[1] * vorticity_phys[2] - velocity_phys[2] * vorticity_phys[1]
    second = velocity_phys[2] * vorticity_phys[0] - velocity_phys[0] * vorticity_phys[2]
    third = velocity_phys[0] * vorticity_phys[1] - velocity_phys[1] * vorticity_phys[0]
    return jnp.stack([first, second, third])


def chain_kernel(position_ref, *refs, group_size):
    group_refs = refs[:group_size]
    sides_ref, out_ref = refs[group_size:]
    slab_count = sides_ref.shape[0]

    def apply(matrix, vectors):
        return lax.dot_general(
            vectors,
            matrix,
            (((1,), (1,)), ((), ())),
            precision=lax.Precision.HIGH,
            preferred_element_type=jnp.float32,
        )

    def solve(position):
        def blocks_of(slab):
            label = (slab + 1) % slab_count
            group_slot = (label % group_size - 1) % group_size
            spot_slot = (label // group_size - position) % group_size
            return group_refs[group_slot].at[spot_slot]

        zero = jnp.zeros(sides_ref.shape[2:], jnp.float32)
        forward_values = [zero, sides_ref[1, 0] + sides_ref[0, 1]]
        for k in range(2, slab_count):
            source = sides_ref[k, 0] + sides_ref[k - 1, 1]
            forward_values.append(source - apply(blocks_of(k)[0], forward_values[-1]))
        after = zero
        for k in range(slab_count - 1, 0, -1):
            blocks = blocks_of(k)
            solved = apply(blocks[2], forward_values[k])
            if k < slab_count - 1:
                solved = solved - apply(blocks[1], after)
            out_ref[k] = jnp.stack([solved, after], axis=1)
            after = solved
        out_ref[0] = jnp.stack([zero, after], axis=1)

    for position in range(group_size):
        pl.when(position_ref[0] == position)(functools.partial(solve, position))


def on_device(
    velocity,
    vorticity,
    lift,
    extend,
    interface_chain_factors,
    pivot_inverse,
    interior_diag,
    node_map,
    *,
    slab_count,
):
    components, planes_dev, line_count, point_total = velocity.shape
    quad_points = 3 * PLANES // 2
    slab_index = lax.axis_index("slab")
    group_size = planes_dev
    group_count = slab_count // group_size
    position = ((slab_index + 1) % slab_count) // group_size

    def slab_of(label):
        return (label - 1) % slab_count

    owners = [slab_of(plane * group_size + 1) for plane in range(planes_dev)]

    blocks = jnp.stack(
        [interface_chain_factors[0], interface_chain_factors[1], pivot_inverse], axis=1
    )
    within = [blocks[position]]
    for offset in range(1, group_count):
        pairs = [
            (
                slab_of(rest + group_size * rank),
                slab_of(rest + group_size * ((rank - offset) % group_count)),
            )
            for rest in range(group_size)
            for rank in range(group_count)
        ]
        within.append(lax.ppermute(blocks[(position - offset) % group_count], "slab", pairs))

    halfway_offsets = jnp.concatenate(
        [jnp.zeros((point_total,), jnp.int32), jnp.full((point_total,), point_total, jnp.int32)]
    )
    row_order = node_map[0] + halfway_offsets
    one_hot = (
        row_order[:, None] == jnp.arange(2 * point_total, dtype=jnp.int32)[None, :]
    ).astype(jnp.bfloat16)
    lift_rows = jnp.einsum(
        "ir,rf->if", one_hot, lift, preferred_element_type=jnp.float32
    ).astype(jnp.bfloat16)
    extend_cols = jnp.einsum(
        "hr,ir->hi", extend, one_hot, preferred_element_type=jnp.float32
    ).astype(jnp.bfloat16)

    inverse, forward = spectral_tables(PLANES, quad_points)
    wavenum = lax.dynamic_slice_in_dim(
        plane_numbers(PLANES), lax.axis_index("mode") * planes_dev, planes_dev
    )
    shifts = plane_shift(wavenum)
    velocity_half = velocity.astype(jnp.bfloat16)
    both_fields = jnp.concatenate([velocity_half, vorticity], axis=0)
    field_lines = lax.all_to_all(both_fields, "mode", split_axis=2, concat_axis=1, tiled=True)
    within, field_lines = lax.optimization_barrier((tuple(within), field_lines))
    group_blocks = jnp.stack(within)
    across = [group_blocks]
    for offset in range(1, group_size):
        pairs = [
            (slab_of(plane * group_size + (1 + offset) % group_size), owners[plane])
            for plane in range(planes_dev)
        ]
        across.append(lax.ppermute(group_blocks, "slab", pairs))
    phys = jnp.einsum("qp,cplb->cqlb", inverse, field_lines, preferred_element_type=jnp.float32)
    lamb_field = lamb_vector(phys[:components], phys[components:]).astype(jnp.bfloat16)
    nonlin_lines = jnp.einsum(
        "pq,cqlb->cplb", forward, lamb_field, preferred_element_type=jnp.float32
    ).astype(jnp.bfloat16)
    interior_point_velocity = (
        (LAMBDA_TIMESTEP * velocity[:, :, 1:, :])
        .astype(jnp.bfloat16)
        .reshape(components, planes_dev, -1)
    )
    lifted_velocity = jnp.einsum(
        "hf,vqf->qvh", lift_rows, interior_point_velocity, preferred_element_type=jnp.float32
    )
    nonlin = lax.all_to_all(nonlin_lines, "mode", split_axis=1, concat_axis=2, tiled=True)
    inner_nonlinear_term = nonlin[:, :, 1:, :].reshape(components, planes_dev, -1)
    cond_line = lifted_velocity + jnp.einsum(
        "hf,vqf->qvh", lift_rows, inner_nonlinear_term, preferred_element_type=jnp.float32
    )
    line_zero_rhs = jnp.swapaxes(
        LAMBDA_TIMESTEP * velocity[:, :, 0, :] + nonlin[:, :, 0, :].astype(jnp.float32), 0, 1
    )
    rhs_left = cond_line[:, :, :point_total] + line_zero_rhs
    right_part = cond_line[:, :, point_total:]

    sides = jnp.stack([rhs_left, right_part], axis=1)
    destination_plane = [owners.index(slab) if slab in owners else 0 for slab in range(slab_count)]
    outgoing = jnp.stack([sides[plane] for plane in destination_plane])
    to_owner = lax.all_to_all(outgoing, "slab", split_axis=0, concat_axis=0, tiled=True)
    both_sides = pl.pallas_call(
        functools.partial(chain_kernel, group_size=group_size),
        out_shape=jax.ShapeDtypeStruct(
            (slab_count, components, 2, point_total), jnp.float32
        ),
        in_specs=[pl.BlockSpec(memory_space=pltpu.SMEM)]
        + [pl.BlockSpec(memory_space=pltpu.VMEM)] * (group_size + 1),
        out_specs=pl.BlockSpec(memory_space=pltpu.VMEM),
    )(position.astype(jnp.int32).reshape(1), *across, to_owner)
    from_owner = lax.all_to_all(both_sides, "slab", split_axis=0, concat_axis=0, tiled=True)
    mine = jnp.stack([from_owner[owner] for owner in owners])
    left_values = mine[:, :, 0]
    right_values = mine[:, :, 1]

    boundary_line = jnp.concatenate([left_values, right_values], axis=2).astype(jnp.bfloat16)
    extension = jnp.einsum(
        "hg,dog->odh", extend_cols, boundary_line, preferred_element_type=jnp.float32
    )
    extension = extension.reshape(components, planes_dev, line_count - 1, point_total)
    inner_rhs = LAMBDA_TIMESTEP * velocity[:, :, 1:, :] + nonlin[:, :, 1:, :].astype(jnp.float32)
    new_inner = extension + inner_rhs / (interior_diag[None, None] + shifts[None, :, None, None])
    line_zero = jnp.swapaxes(left_values, 0, 1)
    return jnp.concatenate([line_zero[:, :, None, :], new_inner], axis=2)


def solution(mesh):
    in_specs = (
        P(None, "mode", "slab", None),
        P(None, "mode", "slab", None),
        P("slab", None),
        P("slab", None),
        P(None, "mode", "slab", None),
        P("mode", "slab", None),
        P("slab", None),
        P("slab", None),
    )
    out_specs = P(None, "mode", "slab", None)
    return jax.shard_map(
        functools.partial(on_device, slab_count=mesh.shape["slab"]), mesh=mesh, in_specs=in_specs, out_specs=out_specs, check_vma=False
    )
```
